32 devices in a mesh: grp: 2 (over x), wide: 16 (over z, y, core).
Axes of the slice: x: 2, y: 2, z: 4, core: 2. Of those that a mesh axis runs over, the one named last changes fastest.
Arguments:
- query_maps: bfloat16 [4096, 1024], P(('grp', 'wide')), parts along dimension 0
- source_maps: bfloat16 [4096, 1024], P(('grp', 'wide')), parts along dimension 0
- hubs: int32 [8], P('grp'), parts along dimension 0, may hold values from 0 to 15, as said below
- pick: int32 [32, 2], P(('grp', 'wide')), parts along dimension 0, may hold values from 0 to 3, all different within a row
- weight_first: bfloat16 [16, 1, 3, 3, 3, 3], replicated, may hold values from -0.625 to 0.625
- bias_first: float32 [16], replicated, may hold values from -0.6 to 0.6
- weight_second: bfloat16 [1, 16, 3, 3, 3, 3], replicated, may hold values from -0.15625 to 0.15625
- bias_second: float32 [1], replicated, may hold values from 0 to 0.2
Outputs:
- consensus: float32 [32, 2, 128, 128], P(('grp', 'wide')), parts along dimension 0
The draws below stay inside these ranges and needn't reach their ends.
There are 2 independent parts, one for each index of `grp`. The reference program is written for one: setup_inputs(seed, part) draws one part's arguments, and reference() takes and returns one part's arrays. A program takes and returns all parts, laid end to end along the dimension named above; an argument that names none is the same for every part. Nothing has to cross between parts.
Inputs may be any that keep to these rules, and one draw needn't show every extreme that they name: `hubs`: distinct photo indices of the batch.
All inputs are finite; a program needn't handle non-finite values.
Results may differ from the reference program's by a relative error of at most 0.0063.
Values may be sent and summed in bfloat16 or wider, within the bound.
No kernel may reach another device: no remote copies, remote signals or barrier semaphores. Data moves between devices by JAX's collectives and lax.ppermute only.
A program may use at most 64 MiB of HBM per device.

```python
import math
import jax
import jax.numpy as jnp
from jax import lax

C = 1024
HQ = 4
WQ = 32
HID = 16
HUBS = 4
CELLS = 128
ROWS = 2048
N_WIDE = 16


def row_features(key, salt):
    book_key = jax.random.fold_in(key, 5)
    own_key = jax.random.fold_in(key, salt)
    code_key, noise_key, scale_key = jax.random.split(own_key, 3)
    book = jax.random.normal(book_key, (16, C), jnp.float32)
    codes = jax.random.randint(code_key, (ROWS,), 0, 16)
    planted = jnp.take(book, codes, axis=0)
    noise = jax.random.normal(noise_key, (ROWS, C), jnp.float32)
    base = 0.8 * planted + 0.6 * noise
    scales = jnp.exp(jax.random.uniform(scale_key, (ROWS, 1), jnp.float32, 0.0, math.log(10.0)))
    return (base * scales).astype(jnp.bfloat16)


def draw_query_maps(key, part):
    return row_features(key, 11)


def draw_source_maps(key, part):
    return row_features(key, 23)


def draw_hubs(key, part):
    inner_key = jax.random.fold_in(key, 37)
    order_key = jax.random.fold_in(key, 41)
    middle = 1 + jax.random.permutation(inner_key, N_WIDE - 2)[:HUBS - 2]
    ends = jnp.array([0, N_WIDE - 1], dtype=jnp.int32)
    values = jnp.concatenate([ends, middle.astype(jnp.int32)])
    return jax.random.permutation(order_key, values).astype(jnp.int32)


def distinct(key, rows, count, top, lift):
    sequence = jax.random.permutation(jax.random.fold_in(key, 1), count)
    favour = sequence
    for power in range(3):
        favour = favour * favour // count
    favour = favour * lift // count
    lots = jax.random.randint(jax.random.fold_in(key, 2), (rows, count), 0, 4096) + favour
    sure = jax.random.permutation(jax.random.fold_in(key, 3), rows)[jnp.arange(count) % rows]
    lots = jnp.where(jnp.arange(rows)[:, None] == sure[None, :], 1 << 14, lots)
    priority = lots * count + jnp.arange(count)
    return lax.top_k(priority.astype(jnp.int32), top)[1].astype(jnp.int32)


def centred(key, extent, deviation, most, kind=jnp.bfloat16):
    values = deviation * jax.random.normal(key, extent, jnp.float32)
    return jnp.clip(values, min=-most, max=most).astype(kind)


def setup_inputs(seed: int = 0, part: int = 0) -> dict:
    splits = jax.random.split(jax.random.key(seed), 9)
    part_keys = jax.random.split(jax.random.fold_in(splits[8], part), 9)
    query_maps = draw_query_maps(jax.random.fold_in(jax.random.fold_in(splits[8], part), 71), part)
    source_maps = draw_source_maps(jax.random.fold_in(jax.random.fold_in(splits[8], part), 71), part)
    hubs = draw_hubs(jax.random.fold_in(jax.random.fold_in(splits[8], part), 71), part)
    pick = distinct(part_keys[3], N_WIDE, HUBS, 2, 8192)
    weight_first = centred(splits[4], (HID, 1, 3, 3, 3, 3), 81 ** -0.5, 0.625)
    bias_first = centred(splits[5], (HID,), 0.2, 0.6, jnp.float32)
    weight_second = centred(splits[6], (1, HID, 3, 3, 3, 3), (81 * HID) ** -0.5, 0.15625)
    bias_second = jnp.clip(jax.random.uniform(splits[7], (1,), jnp.float32, 0.0, 0.2), 0.0, 0.2)
    return dict(query_maps=query_maps, source_maps=source_maps, hubs=hubs, pick=pick, weight_first=weight_first, bias_first=bias_first, weight_second=weight_second, bias_second=bias_second)


def conv_volume(volume, kernel):
    padded = jnp.pad(volume, ((1, 1), (0, 0), (0, 0), (0, 0), (0, 0)))
    height = volume.shape[0]
    result = None
    for offset in range(3):
        term = lax.conv_general_dilated(padded[offset:offset + height], kernel[:, :, offset], (1, 1, 1), [(1, 1), (1, 1), (1, 1)], preferred_element_type=jnp.float32)
        result = term if result is None else result + term
    return result

def consensus_net(matrix, weight_first, bias_first, weight_second, bias_second):
    volume = matrix.reshape(HQ, WQ, HQ, WQ)[:, None]
    preact = conv_volume(volume, weight_first) + bias_first[None, :, None, None, None]
    hidden = jax.nn.relu(preact).astype(jnp.bfloat16)
    result = jax.nn.relu(conv_volume(hidden, weight_second) + bias_second[None, :, None, None, None])
    return result.reshape(CELLS, CELLS)

def scaled_corr(query, sources):
    query_f = query.astype(jnp.float32)
    sources_f = sources.astype(jnp.float32)
    query_rms = jnp.sqrt(lax.optimization_barrier(jnp.mean(query_f * query_f, axis=-1)) + 1e-06)
    source_rms = jnp.sqrt(lax.optimization_barrier(jnp.mean(sources_f * sources_f, axis=-1)) + 1e-06)
    inner = jnp.einsum('ac,jbc->jab', query_f, sources_f, precision=lax.Precision.HIGHEST)
    scale = jnp.sqrt(jnp.float32(C))
    return (inner / (scale * query_rms[None, :, None] * source_rms[:, None, :])).astype(jnp.bfloat16)

def reference(query_maps, source_maps, hubs, pick, weight_first, bias_first, weight_second, bias_second):
    queries = query_maps.reshape(N_WIDE, CELLS, C)
    sources = source_maps.reshape(N_WIDE, CELLS, C)
    owners = hubs[pick]

    def position(index):
        chosen = sources[owners[index]]
        correlation = scaled_corr(queries[index], chosen)
        filtered = []
        for pair in range(2):
            forward = consensus_net(correlation[pair], weight_first, bias_first, weight_second, bias_second)
            backward = consensus_net(correlation[pair].T, weight_first, bias_first, weight_second, bias_second)
            filtered.append(forward + backward.T)
        return jnp.stack(filtered)
    return lax.map(position, jnp.arange(N_WIDE, dtype=jnp.int32))
```

```python
import numpy as np
import jax
import jax.numpy as jnp
from jax import lax
from jax.sharding import PartitionSpec as P

HQ = 4
WQ = 32
TAPS = 9


def spread(value, axis, source):
    kept = jnp.where(lax.axis_index(axis) == source, value, 0).astype(value.dtype)
    return lax.psum(kept, axis)


def tap_onehot():
    cells = HQ * WQ
    table = np.zeros((TAPS, cells, cells), np.float32)
    for b1 in range(HQ):
        for b2 in range(WQ):
            for e1 in range(3):
                for e2 in range(3):
                    p1, p2 = b1 + e1 - 1, b2 + e2 - 1
                    if 0 <= p1 < HQ and 0 <= p2 < WQ:
                        table[e1 * 3 + e2, p1 * WQ + p2, b1 * WQ + b2] = 1.0
    return jnp.asarray(table, jnp.bfloat16)


def row_shifts(x):
    cells = x.shape[1]
    pad = WQ + 1
    padded = jnp.pad(x, ((0, 0), (pad, pad), (0, 0)))
    col = np.arange(cells) % WQ
    outs = []
    for d in range(TAPS):
        d1, d2 = d // 3 - 1, d % 3 - 1
        off = d1 * WQ + d2
        part = lax.slice_in_dim(padded, pad + off, pad + off + cells, axis=1)
        valid = (col + d2 >= 0) & (col + d2 < WQ)
        outs.append(jnp.where(valid[None, :, None], part, jnp.zeros((), x.dtype)))
    return outs


def band_weights(weight_first, weight_second):
    onehot = tap_onehot()
    hid = weight_first.shape[0]
    cells = HQ * WQ
    w1 = weight_first.reshape(hid, TAPS, TAPS)
    w2 = weight_second.reshape(hid, TAPS, TAPS)
    k1 = jnp.einsum("cde,exy->dxcy", w1, onehot, preferred_element_type=jnp.float32)
    k1 = k1.astype(jnp.bfloat16).reshape(TAPS * cells, hid * cells)
    k2 = jnp.einsum("cde,exy->cxdy", w2, onehot, preferred_element_type=jnp.float32)
    k2 = k2.astype(jnp.bfloat16).reshape(hid * cells, TAPS * cells)
    return k1, k2


def consensus_stack(volumes, k1, k2, bias_first, bias_second):
    cells = volumes.shape[1]
    hid = bias_first.shape[0]
    stacked = jnp.concatenate(row_shifts(volumes), axis=-1)
    pre = jnp.einsum("vak,kn->van", stacked, k1, preferred_element_type=jnp.float32)
    pre = pre + jnp.repeat(bias_first, cells)[None, None, :]
    hidden = jax.nn.relu(pre).astype(jnp.bfloat16)
    part = jnp.einsum("vak,kn->van", hidden, k2, preferred_element_type=jnp.float32)
    pieces = [part[:, :, d * cells:(d + 1) * cells] for d in range(TAPS)]
    shifted = []
    for d in range(TAPS):
        shifted.append(row_shifts(pieces[d])[d])
    total = shifted[0]
    for d in range(1, TAPS):
        total = total + shifted[d]
    return jax.nn.relu(total + bias_second[0])


def scaled_corr(query, sources):
    query_f = query.astype(jnp.float32)
    sources_f = sources.astype(jnp.float32)
    query_rms = jnp.sqrt(jnp.mean(query_f * query_f, axis=-1) + 1e-06)
    source_rms = jnp.sqrt(jnp.mean(sources_f * sources_f, axis=-1) + 1e-06)
    inner = jnp.einsum("ac,jbc->jab", query, sources, preferred_element_type=jnp.float32)
    scale = jnp.sqrt(jnp.float32(query.shape[1]))
    return (inner / (scale * query_rms[None, :, None] * source_rms[:, None, :])).astype(
        jnp.bfloat16
    )


def per_device(
    query_maps, source_maps, hubs, pick, weight_first, bias_first, weight_second, bias_second
):
    owners = pick[0]
    cells, channels = source_maps.shape
    chosen = jnp.zeros((2, cells, channels), jnp.bfloat16)
    for index in range(hubs.shape[0]):
        arrived = spread(source_maps, "wide", hubs[index])
        chosen = jnp.where((owners == index)[:, None, None], arrived[None], chosen)
    correlation = scaled_corr(query_maps, chosen)
    volumes = jnp.concatenate([correlation, jnp.swapaxes(correlation, 1, 2)], axis=0)
    k1, k2 = band_weights(weight_first, weight_second)
    filtered = consensus_stack(volumes, k1, k2, bias_first, bias_second)
    return (filtered[:2] + jnp.swapaxes(filtered[2:], 1, 2))[None]


def solution(mesh):
    return jax.shard_map(
        per_device,
        mesh=mesh,
        in_specs=(
            P(("grp", "wide"), None),
            P(("grp", "wide"), None),
            P("grp"),
            P(("grp", "wide"), None),
            P(),
            P(),
            P(),
            P(),
        ),
        out_specs=P(("grp", "wide"), None, None, None),
        check_vma=False,
    )
```

```python
import numpy as np
import jax
import jax.numpy as jnp
from jax import lax
from jax.sharding import PartitionSpec as P

HQ = 4
WQ = 32
TAPS = 9


def tap_table(cells, cols):
    row = lax.broadcasted_iota(jnp.int32, (cells, cols), 0)
    col = lax.broadcasted_iota(jnp.int32, (cells, cols), 1) % cells
    e1 = row // WQ - col // WQ + 1
    e2 = row % WQ - col % WQ + 1
    inside = (e1 >= 0) & (e1 < 3) & (e2 >= 0) & (e2 < 3)
    return jnp.where(inside, e1 * 3 + e2, -1)


def banded(weights, table, cells):
    rows, _, groups = weights.shape
    spread_w = jnp.repeat(weights, cells, axis=2)
    band = jnp.zeros((rows, cells, groups * cells), weights.dtype)
    for e in range(TAPS):
        band = jnp.where(table[None] == e, spread_w[:, e, None, :], band)
    return band


def band_weights(weight_first, weight_second):
    hid = weight_first.shape[0]
    cells = HQ * WQ
    w1 = weight_first.reshape(hid, TAPS, TAPS)
    w2 = weight_second.reshape(hid, TAPS, TAPS)
    k1 = banded(jnp.transpose(w1, (1, 2, 0)), tap_table(cells, hid * cells), cells)
    k1 = k1.reshape(TAPS * cells, hid * cells)
    k2 = banded(jnp.transpose(w2, (0, 2, 1)), tap_table(cells, TAPS * cells), cells)
    k2 = k2.reshape(hid * cells, TAPS * cells)
    return k1, k2


def row_shifts(x):
    cells = x.shape[1]
    pad = WQ + 1
    padded = jnp.pad(x, ((0, 0), (pad, pad), (0, 0)))
    col = np.arange(cells) % WQ
    outs = []
    for d in range(TAPS):
        d1, d2 = d // 3 - 1, d % 3 - 1
        off = d1 * WQ + d2
        part = lax.slice_in_dim(padded, pad + off, pad + off + cells, axis=1)
        valid = (col + d2 >= 0) & (col + d2 < WQ)
        outs.append(jnp.where(valid[None, :, None], part, jnp.zeros((), x.dtype)))
    return outs


def consensus_stack(volumes, k1, k2, bias_first, bias_second):
    cells = volumes.shape[1]
    hid = bias_first.shape[0]
    stacked = jnp.concatenate(row_shifts(volumes), axis=-1)
    pre = jnp.einsum("vak,kn->van", stacked, k1, preferred_element_type=jnp.float32)
    pre = pre + jnp.repeat(bias_first, cells)[None, None, :]
    hidden = jax.nn.relu(pre).astype(jnp.bfloat16)
    part = jnp.einsum("vak,kn->van", hidden, k2, preferred_element_type=jnp.float32)
    pieces = [part[:, :, d * cells:(d + 1) * cells] for d in range(TAPS)]
    shifted = []
    for d in range(TAPS):
        shifted.append(row_shifts(pieces[d])[d])
    total = shifted[0]
    for d in range(1, TAPS):
        total = total + shifted[d]
    return jax.nn.relu(total + bias_second[0])


def scaled_corr(query, sources):
    query_f = query.astype(jnp.float32)
    sources_f = sources.astype(jnp.float32)
    query_rms = jnp.sqrt(jnp.mean(query_f * query_f, axis=-1) + 1e-06)
    source_rms = jnp.sqrt(jnp.mean(sources_f * sources_f, axis=-1) + 1e-06)
    inner = jnp.einsum("ac,jbc->jab", query, sources, preferred_element_type=jnp.float32)
    scale = jnp.sqrt(jnp.float32(query.shape[1]))
    return (inner / (scale * query_rms[None, :, None] * source_rms[:, None, :])).astype(
        jnp.bfloat16
    )


def gather_sources(source_maps, hubs, pick, wide):
    cells, channels = source_maps.shape
    rows = cells // wide
    chunks = lax.all_to_all(source_maps.reshape(wide, rows, channels), "wide", 0, 0)
    picks = lax.all_to_all(jnp.broadcast_to(pick[0][None], (wide, 2)), "wide", 0, 0)
    owners = hubs[picks]
    parcel = chunks[owners]
    got = lax.all_to_all(parcel, "wide", 0, 0)
    return jnp.swapaxes(got, 0, 1).reshape(2, cells, channels)


def per_device(
    query_maps, source_maps, hubs, pick, weight_first, bias_first, weight_second, bias_second,
    wide,
):
    chosen = gather_sources(source_maps, hubs, pick, wide)
    correlation = scaled_corr(query_maps, chosen)
    volumes = jnp.concatenate([correlation, jnp.swapaxes(correlation, 1, 2)], axis=0)
    k1, k2 = band_weights(weight_first, weight_second)
    filtered = consensus_stack(volumes, k1, k2, bias_first, bias_second)
    return (filtered[:2] + jnp.swapaxes(filtered[2:], 1, 2))[None]


def solution(mesh):
    wide = mesh.shape["wide"]

    def body(*args):
        return per_device(*args, wide)

    return jax.shard_map(
        body,
        mesh=mesh,
        in_specs=(
            P(("grp", "wide"), None),
            P(("grp", "wide"), None),
            P("grp"),
            P(("grp", "wide"), None),
            P(),
            P(),
            P(),
            P(),
        ),
        out_specs=P(("grp", "wide"), None, None, None),
        check_vma=False,
    )
```

```python
import numpy as np
import jax
import jax.numpy as jnp
from jax import lax
from jax.sharding import PartitionSpec as P

HQ = 4
WQ = 32
TAPS = 9


def tap_table(cells, cols):
    row = lax.broadcasted_iota(jnp.int32, (cells, cols), 0)
    col = lax.broadcasted_iota(jnp.int32, (cells, cols), 1) % cells
    e1 = row // WQ - col // WQ + 1
    e2 = row % WQ - col % WQ + 1
    inside = (e1 >= 0) & (e1 < 3) & (e2 >= 0) & (e2 < 3)
    return jnp.where(inside, e1 * 3 + e2, -1)


def banded(weights, table, cells):
    rows, _, groups = weights.shape
    spread_w = jnp.repeat(weights, cells, axis=2)
    band = jnp.zeros((rows, cells, groups * cells), weights.dtype)
    for e in range(TAPS):
        band = jnp.where(table[None] == e, spread_w[:, e, None, :], band)
    return band


def band_weights(weight_first, weight_second):
    hid = weight_first.shape[0]
    cells = HQ * WQ
    w1 = weight_first.reshape(hid, TAPS, TAPS)
    w2 = weight_second.reshape(hid, TAPS, TAPS)
    k1 = banded(jnp.transpose(w1, (1, 2, 0)), tap_table(cells, hid * cells), cells)
    k1 = k1.reshape(TAPS * cells, hid * cells)
    k2 = banded(jnp.transpose(w2, (0, 2, 1)), tap_table(cells, TAPS * cells), cells)
    k2 = k2.reshape(hid * cells, TAPS * cells)
    return k1, k2


def row_shifts(x):
    cells = x.shape[1]
    pad = WQ + 1
    padded = jnp.pad(x, ((0, 0), (pad, pad), (0, 0)))
    col = np.arange(cells) % WQ
    outs = []
    for d in range(TAPS):
        d1, d2 = d // 3 - 1, d % 3 - 1
        off = d1 * WQ + d2
        part = lax.slice_in_dim(padded, pad + off, pad + off + cells, axis=1)
        valid = (col + d2 >= 0) & (col + d2 < WQ)
        outs.append(jnp.where(valid[None, :, None], part, jnp.zeros((), x.dtype)))
    return outs


def consensus_stack(volumes, k1, k2, bias_first, bias_second):
    cells = volumes.shape[1]
    hid = bias_first.shape[0]
    stacked = jnp.concatenate(row_shifts(volumes), axis=-1)
    pre = jnp.einsum("vak,kn->van", stacked, k1, preferred_element_type=jnp.float32)
    pre = pre + jnp.repeat(bias_first, cells)[None, None, :]
    hidden = jax.nn.relu(pre).astype(jnp.bfloat16)
    part = jnp.einsum("vak,kn->van", hidden, k2, preferred_element_type=jnp.float32)
    pieces = [part[:, :, d * cells:(d + 1) * cells] for d in range(TAPS)]
    shifted = []
    for d in range(TAPS):
        shifted.append(row_shifts(pieces[d])[d])
    total = shifted[0]
    for d in range(1, TAPS):
        total = total + shifted[d]
    return jax.nn.relu(total + bias_second[0])


def scaled_corr(query, sources):
    query_f = query.astype(jnp.float32)
    sources_f = sources.astype(jnp.float32)
    query_rms = jnp.sqrt(jnp.mean(query_f * query_f, axis=-1) + 1e-06)
    source_rms = jnp.sqrt(jnp.mean(sources_f * sources_f, axis=-1) + 1e-06)
    inner = jnp.einsum("ac,jbc->jab", query, sources, preferred_element_type=jnp.float32)
    scale = jnp.sqrt(jnp.float32(query.shape[1]))
    return (inner / (scale * query_rms[None, :, None] * source_rms[:, None, :])).astype(
        jnp.bfloat16
    )


def gather_sources(source_maps, hubs, pick, wide):
    cells, channels = source_maps.shape
    rows = cells // wide
    lanes = 128
    tag = jnp.zeros((wide, rows, lanes), source_maps.dtype)
    tag = tag.at[:, 0, :2].set(pick[0][None, :].astype(source_maps.dtype))
    payload = jnp.concatenate([source_maps.reshape(wide, rows, channels), tag], axis=2)
    arrived = lax.all_to_all(payload, "wide", 0, 0)
    chunks = arrived[:, :, :channels]
    picks = arrived[:, 0, channels:channels + 2].astype(jnp.int32)
    owners = hubs[picks]
    parcel = chunks[owners]
    got = lax.all_to_all(parcel, "wide", 0, 0)
    return jnp.swapaxes(got, 0, 1).reshape(2, cells, channels)


def per_device(
    query_maps, source_maps, hubs, pick, weight_first, bias_first, weight_second, bias_second,
    wide,
):
    chosen = gather_sources(source_maps, hubs, pick, wide)
    correlation = scaled_corr(query_maps, chosen)
    volumes = jnp.concatenate([correlation, jnp.swapaxes(correlation, 1, 2)], axis=0)
    k1, k2 = band_weights(weight_first, weight_second)
    filtered = consensus_stack(volumes, k1, k2, bias_first, bias_second)
    return (filtered[:2] + jnp.swapaxes(filtered[2:], 1, 2))[None]


def solution(mesh):
    wide = mesh.shape["wide"]

    def body(*args):
        return per_device(*args, wide)

    return jax.shard_map(
        body,
        mesh=mesh,
        in_specs=(
            P(("grp", "wide"), None),
            P(("grp", "wide"), None),
            P("grp"),
            P(("grp", "wide"), None),
            P(),
            P(),
            P(),
            P(),
        ),
        out_specs=P(("grp", "wide"), None, None, None),
        check_vma=False,
    )
```

```python
import numpy as np
import jax
import jax.numpy as jnp
from jax import lax
from jax.sharding import PartitionSpec as P

HQ = 4
WQ = 32
TAPS = 9


def tap_table(cells, cols):
    row = lax.broadcasted_iota(jnp.int32, (cells, cols), 0)
    col = lax.broadcasted_iota(jnp.int32, (cells, cols), 1) % cells
    e1 = row // WQ - col // WQ + 1
    e2 = row % WQ - col % WQ + 1
    inside = (e1 >= 0) & (e1 < 3) & (e2 >= 0) & (e2 < 3)
    return jnp.where(inside, e1 * 3 + e2, -1)


def banded(weights, table, cells):
    rows, _, groups = weights.shape
    spread_w = jnp.repeat(weights, cells, axis=2)
    band = jnp.zeros((rows, cells, groups * cells), weights.dtype)
    for e in range(TAPS):
        band = jnp.where(table[None] == e, spread_w[:, e, None, :], band)
    return band


def band_weights(weight_first, weight_second):
    hid = weight_first.shape[0]
    cells = HQ * WQ
    w1 = weight_first.reshape(hid, TAPS, TAPS)
    w2 = weight_second.reshape(hid, TAPS, TAPS)
    k1 = banded(jnp.transpose(w1, (1, 2, 0)), tap_table(cells, hid * cells), cells)
    k1 = k1.reshape(TAPS * cells, hid * cells)
    k2 = banded(jnp.transpose(w2, (0, 2, 1)), tap_table(cells, TAPS * cells), cells)
    k2 = k2.reshape(hid * cells, TAPS * cells)
    return k1, k2


def row_shifts(x):
    cells = x.shape[1]
    pad = WQ + 1
    padded = jnp.pad(x, ((0, 0), (pad, pad), (0, 0)))
    col = np.arange(cells) % WQ
    outs = []
    for d in range(TAPS):
        d1, d2 = d // 3 - 1, d % 3 - 1
        off = d1 * WQ + d2
        part = lax.slice_in_dim(padded, pad + off, pad + off + cells, axis=1)
        valid = (col + d2 >= 0) & (col + d2 < WQ)
        outs.append(jnp.where(valid[None, :, None], part, jnp.zeros((), x.dtype)))
    return outs


def consensus_stack(volumes, k1, k2, bias_first, bias_second):
    cells = volumes.shape[1]
    hid = bias_first.shape[0]
    stacked = jnp.concatenate(row_shifts(volumes), axis=-1)
    pre = jnp.einsum("vak,kn->van", stacked, k1, preferred_element_type=jnp.float32)
    pre = pre + jnp.repeat(bias_first, cells)[None, None, :]
    hidden = jax.nn.relu(pre).astype(jnp.bfloat16)
    part = jnp.einsum("vak,kn->van", hidden, k2, preferred_element_type=jnp.float32)
    pieces = [part[:, :, d * cells:(d + 1) * cells] for d in range(TAPS)]
    shifted = []
    for d in range(TAPS):
        shifted.append(row_shifts(pieces[d])[d])
    total = shifted[0]
    for d in range(1, TAPS):
        total = total + shifted[d]
    return jax.nn.relu(total + bias_second[0])


def scaled_corr(query, sources):
    query_f = query.astype(jnp.float32)
    sources_f = sources.astype(jnp.float32)
    query_rms = jnp.sqrt(jnp.mean(query_f * query_f, axis=-1) + 1e-06)
    source_rms = jnp.sqrt(jnp.mean(sources_f * sources_f, axis=-1) + 1e-06)
    inner = jnp.einsum("ac,jbc->jab", query, sources, preferred_element_type=jnp.float32)
    scale = jnp.sqrt(jnp.float32(query.shape[1]))
    return (inner / (scale * query_rms[None, :, None] * source_rms[:, None, :])).astype(
        jnp.bfloat16
    )


def gather_sources(source_maps, hubs, pick, wide):
    cells, channels = source_maps.shape
    rows = cells // wide
    lanes = 128
    tag = jnp.zeros((wide, rows, lanes), source_maps.dtype)
    tag = tag.at[:, 0, :2].set(pick[0][None, :].astype(source_maps.dtype))
    payload = jnp.concatenate([source_maps.reshape(wide, rows, channels), tag], axis=2)
    arrived = lax.all_to_all(payload, "wide", 0, 0)
    chunks = arrived[:, :, :channels]
    picks = arrived[:, 0, channels:channels + 2].astype(jnp.int32)
    owners = hubs[picks]
    parcel = chunks[owners]
    got = lax.all_to_all(parcel, "wide", 0, 0)
    return jnp.swapaxes(got, 0, 1).reshape(2, cells, channels), parcel


def per_device(
    query_maps, source_maps, hubs, pick, weight_first, bias_first, weight_second, bias_second,
    wide,
):
    chosen, parcel = gather_sources(source_maps, hubs, pick, wide)
    correlation = scaled_corr(query_maps, chosen)
    volumes = jnp.concatenate([correlation, jnp.swapaxes(correlation, 1, 2)], axis=0)
    weight_first, weight_second, _ = lax.optimization_barrier(
        (weight_first, weight_second, parcel)
    )
    k1, k2 = band_weights(weight_first, weight_second)
    filtered = consensus_stack(volumes, k1, k2, bias_first, bias_second)
    return (filtered[:2] + jnp.swapaxes(filtered[2:], 1, 2))[None]


def solution(mesh):
    wide = mesh.shape["wide"]

    def body(*args):
        return per_device(*args, wide)

    return jax.shard_map(
        body,
        mesh=mesh,
        in_specs=(
            P(("grp", "wide"), None),
            P(("grp", "wide"), None),
            P("grp"),
            P(("grp", "wide"), None),
            P(),
            P(),
            P(),
            P(),
        ),
        out_specs=P(("grp", "wide"), None, None, None),
        check_vma=False,
    )
```

```python
import numpy as np
import jax
import jax.numpy as jnp
from jax import lax
from jax.sharding import PartitionSpec as P

HQ = 4
WQ = 32
TAPS = 9


def tap_table(cells, cols):
    row = lax.broadcasted_iota(jnp.int32, (cells, cols), 0)
    col = lax.broadcasted_iota(jnp.int32, (cells, cols), 1) % cells
    e1 = row // WQ - col // WQ + 1
    e2 = row % WQ - col % WQ + 1
    inside = (e1 >= 0) & (e1 < 3) & (e2 >= 0) & (e2 < 3)
    return jnp.where(inside, e1 * 3 + e2, -1)


def banded(weights, table, cells):
    rows, _, groups = weights.shape
    spread_w = jnp.repeat(weights, cells, axis=2)
    band = jnp.zeros((rows, cells, groups * cells), weights.dtype)
    for e in range(TAPS):
        band = jnp.where(table[None] == e, spread_w[:, e, None, :], band)
    return band


def band_weights(weight_first, weight_second, tie):
    hid = weight_first.shape[0]
    cells = HQ * WQ
    w1 = weight_first.reshape(hid, TAPS, TAPS)
    k1 = banded(jnp.transpose(w1, (1, 2, 0)), tap_table(cells, hid * cells), cells)
    k1 = k1.reshape(TAPS * cells, hid * cells)
    table, weight_second, _ = lax.optimization_barrier(
        (tap_table(cells, TAPS * cells), weight_second, tie)
    )
    w2 = weight_second.reshape(hid, TAPS, TAPS)
    k2 = banded(jnp.transpose(w2, (0, 2, 1)), table, cells)
    k2 = k2.reshape(hid * cells, TAPS * cells)
    return k1, k2


def row_shifts(x):
    cells = x.shape[1]
    pad = WQ + 1
    padded = jnp.pad(x, ((0, 0), (pad, pad), (0, 0)))
    col = np.arange(cells) % WQ
    outs = []
    for d in range(TAPS):
        d1, d2 = d // 3 - 1, d % 3 - 1
        off = d1 * WQ + d2
        part = lax.slice_in_dim(padded, pad + off, pad + off + cells, axis=1)
        valid = (col + d2 >= 0) & (col + d2 < WQ)
        outs.append(jnp.where(valid[None, :, None], part, jnp.zeros((), x.dtype)))
    return outs


def consensus_stack(volumes, k1, k2, bias_first, bias_second):
    cells = volumes.shape[1]
    hid = bias_first.shape[0]
    stacked = jnp.concatenate(row_shifts(volumes), axis=-1)
    pre = jnp.einsum("vak,kn->van", stacked, k1, preferred_element_type=jnp.float32)
    pre = pre + jnp.repeat(bias_first, cells)[None, None, :]
    hidden = jax.nn.relu(pre).astype(jnp.bfloat16)
    part = jnp.einsum("vak,kn->van", hidden, k2, preferred_element_type=jnp.float32)
    pieces = [part[:, :, d * cells:(d + 1) * cells] for d in range(TAPS)]
    shifted = []
    for d in range(TAPS):
        shifted.append(row_shifts(pieces[d])[d])
    total = shifted[0]
    for d in range(1, TAPS):
        total = total + shifted[d]
    return jax.nn.relu(total + bias_second[0])


def scaled_corr(query, sources):
    query_f = query.astype(jnp.float32)
    sources_f = sources.astype(jnp.float32)
    query_rms = jnp.sqrt(jnp.mean(query_f * query_f, axis=-1) + 1e-06)
    source_rms = jnp.sqrt(jnp.mean(sources_f * sources_f, axis=-1) + 1e-06)
    inner = jnp.einsum("ac,jbc->jab", query, sources, preferred_element_type=jnp.float32)
    scale = jnp.sqrt(jnp.float32(query.shape[1]))
    return (inner / (scale * query_rms[None, :, None] * source_rms[:, None, :])).astype(
        jnp.bfloat16
    )


def gather_sources(source_maps, hubs, pick, wide):
    cells, channels = source_maps.shape
    rows = cells // wide
    lanes = 128
    tag = jnp.zeros((wide, rows, lanes), source_maps.dtype)
    tag = tag.at[:, 0, :2].set(pick[0][None, :].astype(source_maps.dtype))
    payload = jnp.concatenate([source_maps.reshape(wide, rows, channels), tag], axis=2)
    arrived = lax.all_to_all(payload, "wide", 0, 0)
    chunks = arrived[:, :, :channels]
    picks = arrived[:, 0, channels:channels + 2].astype(jnp.int32)
    owners = hubs[picks]
    parcel = chunks[owners]
    got = lax.all_to_all(parcel, "wide", 0, 0)
    return jnp.swapaxes(got, 0, 1).reshape(2, cells, channels), parcel


def per_device(
    query_maps, source_maps, hubs, pick, weight_first, bias_first, weight_second, bias_second,
    wide,
):
    chosen, parcel = gather_sources(source_maps, hubs, pick, wide)
    correlation = scaled_corr(query_maps, chosen)
    volumes = jnp.concatenate([correlation, jnp.swapaxes(correlation, 1, 2)], axis=0)
    k1, k2 = band_weights(weight_first, weight_second, parcel)
    filtered = consensus_stack(volumes, k1, k2, bias_first, bias_second)
    return (filtered[:2] + jnp.swapaxes(filtered[2:], 1, 2))[None]


def solution(mesh):
    wide = mesh.shape["wide"]

    def body(*args):
        return per_device(*args, wide)

    return jax.shard_map(
        body,
        mesh=mesh,
        in_specs=(
            P(("grp", "wide"), None),
            P(("grp", "wide"), None),
            P("grp"),
            P(("grp", "wide"), None),
            P(),
            P(),
            P(),
            P(),
        ),
        out_specs=P(("grp", "wide"), None, None, None),
        check_vma=False,
    )
```

```python
import numpy as np
import jax
import jax.numpy as jnp
from jax import lax
from jax.sharding import PartitionSpec as P

HQ = 4
WQ = 32
TAPS = 9


def tap_table(cells, cols):
    row = lax.broadcasted_iota(jnp.int32, (cells, cols), 0)
    col = lax.broadcasted_iota(jnp.int32, (cells, cols), 1) % cells
    e1 = row // WQ - col // WQ + 1
    e2 = row % WQ - col % WQ + 1
    inside = (e1 >= 0) & (e1 < 3) & (e2 >= 0) & (e2 < 3)
    return jnp.where(inside, e1 * 3 + e2, -1)


def banded(weights, table, cells):
    rows, _, groups = weights.shape
    spread_w = jnp.repeat(weights, cells, axis=2)
    band = jnp.zeros((rows, cells, groups * cells), weights.dtype)
    for e in range(TAPS):
        band = jnp.where(table[None] == e, spread_w[:, e, None, :], band)
    return band


def band_weights(weight_first, weight_second, tie):
    hid = weight_first.shape[0]
    cells = HQ * WQ
    w1 = weight_first.reshape(hid, TAPS, TAPS)
    k1 = banded(jnp.transpose(w1, (1, 2, 0)), tap_table(cells, hid * cells), cells)
    k1 = k1.reshape(TAPS * cells, hid * cells)
    table, weight_second, _ = lax.optimization_barrier(
        (tap_table(cells, TAPS * cells), weight_second, tie)
    )
    w2 = weight_second.reshape(hid, TAPS, TAPS)
    k2 = banded(jnp.transpose(w2, (0, 2, 1)), table, cells)
    k2 = k2.reshape(hid * cells, TAPS * cells)
    return k1, k2


def row_shifts(x):
    cells = x.shape[1]
    pad = WQ + 1
    padded = jnp.pad(x, ((0, 0), (pad, pad), (0, 0)))
    col = np.arange(cells) % WQ
    outs = []
    for d in range(TAPS):
        d1, d2 = d // 3 - 1, d % 3 - 1
        off = d1 * WQ + d2
        part = lax.slice_in_dim(padded, pad + off, pad + off + cells, axis=1)
        valid = (col + d2 >= 0) & (col + d2 < WQ)
        outs.append(jnp.where(valid[None, :, None], part, jnp.zeros((), x.dtype)))
    return outs


def consensus_stack(volumes, k1, k2, bias_first, bias_second):
    cells = volumes.shape[1]
    hid = bias_first.shape[0]
    stacked = jnp.concatenate(row_shifts(volumes), axis=-1)
    pre = jnp.einsum("vak,kn->van", stacked, k1, preferred_element_type=jnp.float32)
    pre = pre + jnp.repeat(bias_first, cells)[None, None, :]
    hidden = jax.nn.relu(pre).astype(jnp.bfloat16)
    part = jnp.einsum("vak,kn->van", hidden, k2, preferred_element_type=jnp.float32)
    pieces = [part[:, :, d * cells:(d + 1) * cells] for d in range(TAPS)]
    shifted = []
    for d in range(TAPS):
        shifted.append(row_shifts(pieces[d])[d])
    total = shifted[0]
    for d in range(1, TAPS):
        total = total + shifted[d]
    return jax.nn.relu(total + bias_second[0])


def scaled_corr(query, sources):
    query_f = query.astype(jnp.float32)
    sources_f = sources.astype(jnp.float32)
    query_rms = jnp.sqrt(jnp.mean(query_f * query_f, axis=-1) + 1e-06)
    source_rms = jnp.sqrt(jnp.mean(sources_f * sources_f, axis=-1) + 1e-06)
    inner = jnp.einsum("ac,jbc->jab", query, sources, preferred_element_type=jnp.float32)
    scale = jnp.sqrt(jnp.float32(query.shape[1]))
    return (inner / (scale * query_rms[None, :, None] * source_rms[:, None, :])).astype(
        jnp.bfloat16
    )


def gather_sources(source_maps, hubs, pick, sub):
    cells, channels = source_maps.shape
    rows = cells // sub
    lanes = 128
    tag = jnp.zeros((sub, rows, lanes), source_maps.dtype)
    tag = tag.at[:, 0, :2].set(pick[0][None, :].astype(source_maps.dtype))
    payload = jnp.concatenate([source_maps.reshape(sub, rows, channels), tag], axis=2)
    arrived = lax.all_to_all(payload, "sub", 0, 0)
    chunks = arrived[:, :, :channels]
    picks = arrived[:, 0, channels:channels + 2].astype(jnp.int32)
    mine = lax.axis_index("half")
    local = chunks[hubs % sub]
    mirror = lax.ppermute(local, "half", [(0, 1), (1, 0)])
    here = (hubs // sub == mine)[:, None, None]
    named = jnp.where(here, local, mirror)
    parcel = named[picks]
    got = lax.all_to_all(parcel, "sub", 0, 0)
    return jnp.swapaxes(got, 0, 1).reshape(2, cells, channels), parcel


def per_device(
    query_maps, source_maps, hubs, pick, weight_first, bias_first, weight_second, bias_second,
    sub,
):
    chosen, parcel = gather_sources(source_maps, hubs, pick, sub)
    correlation = scaled_corr(query_maps, chosen)
    volumes = jnp.concatenate([correlation, jnp.swapaxes(correlation, 1, 2)], axis=0)
    k1, k2 = band_weights(weight_first, weight_second, parcel)
    filtered = consensus_stack(volumes, k1, k2, bias_first, bias_second)
    return (filtered[:2] + jnp.swapaxes(filtered[2:], 1, 2))[None]


def solution(mesh):
    groups, wide = mesh.shape["grp"], mesh.shape["wide"]
    sub = wide // 2
    split = jax.sharding.Mesh(mesh.devices.reshape(groups, 2, sub), ("grp", "half", "sub"))
    spread = ("grp", "half", "sub")

    def body(*args):
        return per_device(*args, sub)

    return jax.shard_map(
        body,
        mesh=split,
        in_specs=(
            P(spread, None),
            P(spread, None),
            P("grp"),
            P(spread, None),
            P(),
            P(),
            P(),
            P(),
        ),
        out_specs=P(spread, None, None, None),
        check_vma=False,
    )
```

```python
import numpy as np
import jax
import jax.numpy as jnp
from jax import lax
from jax.sharding import PartitionSpec as P

HQ = 4
WQ = 32
TAPS = 9


def tap_table(cells, cols):
    row = lax.broadcasted_iota(jnp.int32, (cells, cols), 0)
    col = lax.broadcasted_iota(jnp.int32, (cells, cols), 1) % cells
    e1 = row // WQ - col // WQ + 1
    e2 = row % WQ - col % WQ + 1
    inside = (e1 >= 0) & (e1 < 3) & (e2 >= 0) & (e2 < 3)
    return jnp.where(inside, e1 * 3 + e2, -1)


def banded(weights, table, cells):
    rows, _, groups = weights.shape
    spread_w = jnp.repeat(weights, cells, axis=2)
    band = jnp.zeros((rows, cells, groups * cells), weights.dtype)
    for e in range(TAPS):
        band = jnp.where(table[None] == e, spread_w[:, e, None, :], band)
    return band


def band_weights(weight_first, weight_second, tie):
    hid = weight_first.shape[0]
    cells = HQ * WQ
    w1 = weight_first.reshape(hid, TAPS, TAPS)
    k1 = banded(jnp.transpose(w1, (1, 2, 0)), tap_table(cells, hid * cells), cells)
    k1 = k1.reshape(TAPS * cells, hid * cells)
    table, weight_second, _ = lax.optimization_barrier(
        (tap_table(cells, TAPS * cells), weight_second, tie)
    )
    w2 = weight_second.reshape(hid, TAPS, TAPS)
    k2 = banded(jnp.transpose(w2, (0, 2, 1)), table, cells)
    k2 = k2.reshape(hid * cells, TAPS * cells)
    return k1, k2


def row_shifts(x):
    cells = x.shape[1]
    pad = WQ + 1
    padded = jnp.pad(x, ((0, 0), (pad, pad), (0, 0)))
    col = np.arange(cells) % WQ
    outs = []
    for d in range(TAPS):
        d1, d2 = d // 3 - 1, d % 3 - 1
        off = d1 * WQ + d2
        part = lax.slice_in_dim(padded, pad + off, pad + off + cells, axis=1)
        valid = (col + d2 >= 0) & (col + d2 < WQ)
        outs.append(jnp.where(valid[None, :, None], part, jnp.zeros((), x.dtype)))
    return outs


def consensus_stack(volumes, k1, k2, bias_first, bias_second):
    cells = volumes.shape[1]
    hid = bias_first.shape[0]
    stacked = jnp.concatenate(row_shifts(volumes), axis=-1)
    pre = jnp.einsum("vak,kn->van", stacked, k1, preferred_element_type=jnp.float32)
    pre = pre + jnp.repeat(bias_first, cells)[None, None, :]
    hidden = jax.nn.relu(pre).astype(jnp.bfloat16)
    part = jnp.einsum("vak,kn->van", hidden, k2, preferred_element_type=jnp.float32)
    pieces = [part[:, :, d * cells:(d + 1) * cells] for d in range(TAPS)]
    shifted = []
    for d in range(TAPS):
        shifted.append(row_shifts(pieces[d])[d])
    total = shifted[0]
    for d in range(1, TAPS):
        total = total + shifted[d]
    return jax.nn.relu(total + bias_second[0])


def scaled_corr(query, sources):
    query_f = query.astype(jnp.float32)
    sources_f = sources.astype(jnp.float32)
    query_rms = jnp.sqrt(jnp.mean(query_f * query_f, axis=-1) + 1e-06)
    source_rms = jnp.sqrt(jnp.mean(sources_f * sources_f, axis=-1) + 1e-06)
    inner = jnp.einsum("ac,jbc->jab", query, sources, preferred_element_type=jnp.float32)
    scale = jnp.sqrt(jnp.float32(query.shape[1]))
    return (inner / (scale * query_rms[None, :, None] * source_rms[:, None, :])).astype(
        jnp.bfloat16
    )


def gather_sources(source_maps, hubs, pick, sub, build):
    cells, channels = source_maps.shape
    rows = cells // sub
    lanes = 128
    tag = jnp.zeros((sub, rows, lanes), source_maps.dtype)
    tag = tag.at[:, 0, :2].set(pick[0][None, :].astype(source_maps.dtype))
    payload = jnp.concatenate([source_maps.reshape(sub, rows, channels), tag], axis=2)
    arrived = lax.all_to_all(payload, "sub", 0, 0)
    chunks = arrived[:, :, :channels]
    picks = arrived[:, 0, channels:channels + 2].astype(jnp.int32)
    mine = lax.axis_index("half")
    local = chunks[hubs % sub]
    mirror = lax.ppermute(local, "half", [(0, 1), (1, 0)])
    bands = build(local)
    mirror, bands = lax.optimization_barrier((mirror, bands))
    here = (hubs // sub == mine)[:, None, None]
    named = jnp.where(here, local, mirror)
    parcel = named[picks]
    got = lax.all_to_all(parcel, "sub", 0, 0)
    return jnp.swapaxes(got, 0, 1).reshape(2, cells, channels), bands


def per_device(
    query_maps, source_maps, hubs, pick, weight_first, bias_first, weight_second, bias_second,
    sub,
):
    chosen, (k1, k2) = gather_sources(
        source_maps, hubs, pick, sub,
        lambda tie: band_weights(weight_first, weight_second, tie),
    )
    correlation = scaled_corr(query_maps, chosen)
    volumes = jnp.concatenate([correlation, jnp.swapaxes(correlation, 1, 2)], axis=0)
    filtered = consensus_stack(volumes, k1, k2, bias_first, bias_second)
    return (filtered[:2] + jnp.swapaxes(filtered[2:], 1, 2))[None]


def solution(mesh):
    groups, wide = mesh.shape["grp"], mesh.shape["wide"]
    sub = wide // 2
    split = jax.sharding.Mesh(mesh.devices.reshape(groups, 2, sub), ("grp", "half", "sub"))
    spread = ("grp", "half", "sub")

    def body(*args):
        return per_device(*args, sub)

    return jax.shard_map(
        body,
        mesh=split,
        in_specs=(
            P(spread, None),
            P(spread, None),
            P("grp"),
            P(spread, None),
            P(),
            P(),
            P(),
            P(),
        ),
        out_specs=P(spread, None, None, None),
        check_vma=False,
    )
```

```python
import numpy as np
import jax
import jax.numpy as jnp
from jax import lax
from jax.sharding import PartitionSpec as P

HQ = 4
WQ = 32
TAPS = 9


def tap_table(cells, cols):
    row = lax.broadcasted_iota(jnp.int32, (cells, cols), 0)
    col = lax.broadcasted_iota(jnp.int32, (cells, cols), 1) % cells
    e1 = row // WQ - col // WQ + 1
    e2 = row % WQ - col % WQ + 1
    inside = (e1 >= 0) & (e1 < 3) & (e2 >= 0) & (e2 < 3)
    return jnp.where(inside, e1 * 3 + e2, -1)


def banded(weights, table, cells):
    rows, _, groups = weights.shape
    spread_w = jnp.repeat(weights, cells, axis=2)
    band = jnp.zeros((rows, cells, groups * cells), weights.dtype)
    for e in range(TAPS):
        band = jnp.where(table[None] == e, spread_w[:, e, None, :], band)
    return band


def band_first(weight_first, tie):
    hid = weight_first.shape[0]
    cells = HQ * WQ
    table, weight_first, _ = lax.optimization_barrier(
        (tap_table(cells, hid * cells), weight_first, tie)
    )
    w1 = weight_first.reshape(hid, TAPS, TAPS)
    k1 = banded(jnp.transpose(w1, (1, 2, 0)), table, cells)
    return k1.reshape(TAPS * cells, hid * cells)


def band_second(weight_second, tie):
    hid = weight_second.shape[1]
    cells = HQ * WQ
    table, weight_second, _ = lax.optimization_barrier(
        (tap_table(cells, TAPS * cells), weight_second, tie)
    )
    w2 = weight_second.reshape(hid, TAPS, TAPS)
    k2 = banded(jnp.transpose(w2, (0, 2, 1)), table, cells)
    return k2.reshape(hid * cells, TAPS * cells)


def row_shifts(x):
    cells = x.shape[1]
    pad = WQ + 1
    padded = jnp.pad(x, ((0, 0), (pad, pad), (0, 0)))
    col = np.arange(cells) % WQ
    outs = []
    for d in range(TAPS):
        d1, d2 = d // 3 - 1, d % 3 - 1
        off = d1 * WQ + d2
        part = lax.slice_in_dim(padded, pad + off, pad + off + cells, axis=1)
        valid = (col + d2 >= 0) & (col + d2 < WQ)
        outs.append(jnp.where(valid[None, :, None], part, jnp.zeros((), x.dtype)))
    return outs


def consensus_stack(volumes, k1, k2, bias_first, bias_second):
    cells = volumes.shape[1]
    hid = bias_first.shape[0]
    stacked = jnp.concatenate(row_shifts(volumes), axis=-1)
    pre = jnp.einsum("vak,kn->van", stacked, k1, preferred_element_type=jnp.float32)
    pre = pre + jnp.repeat(bias_first, cells)[None, None, :]
    hidden = jax.nn.relu(pre).astype(jnp.bfloat16)
    part = jnp.einsum("vak,kn->van", hidden, k2, preferred_element_type=jnp.float32)
    pieces = [part[:, :, d * cells:(d + 1) * cells] for d in range(TAPS)]
    shifted = []
    for d in range(TAPS):
        shifted.append(row_shifts(pieces[d])[d])
    total = shifted[0]
    for d in range(1, TAPS):
        total = total + shifted[d]
    return jax.nn.relu(total + bias_second[0])


def scaled_corr(query, sources):
    query_f = query.astype(jnp.float32)
    sources_f = sources.astype(jnp.float32)
    query_rms = jnp.sqrt(jnp.mean(query_f * query_f, axis=-1) + 1e-06)
    source_rms = jnp.sqrt(jnp.mean(sources_f * sources_f, axis=-1) + 1e-06)
    inner = jnp.einsum("ac,jbc->jab", query, sources, preferred_element_type=jnp.float32)
    scale = jnp.sqrt(jnp.float32(query.shape[1]))
    return (inner / (scale * query_rms[None, :, None] * source_rms[:, None, :])).astype(
        jnp.bfloat16
    )


def gather_sources(source_maps, hubs, pick, sub, weight_first):
    cells, channels = source_maps.shape
    rows = cells // sub
    lanes = 128
    tag = jnp.zeros((sub, rows, lanes), source_maps.dtype)
    tag = tag.at[:, 0, :2].set(pick[0][None, :].astype(source_maps.dtype))
    payload = jnp.concatenate([source_maps.reshape(sub, rows, channels), tag], axis=2)
    arrived = lax.all_to_all(payload, "sub", 0, 0)
    chunks = arrived[:, :, :channels]
    picks = arrived[:, 0, channels:channels + 2].astype(jnp.int32)
    mine = lax.axis_index("half")
    local = chunks[hubs % sub]
    mirror = lax.ppermute(local, "half", [(0, 1), (1, 0)])
    k1 = band_first(weight_first, local)
    mirror, k1 = lax.optimization_barrier((mirror, k1))
    here = (hubs // sub == mine)[:, None, None]
    named = jnp.where(here, local, mirror)
    parcel = named[picks]
    got = lax.all_to_all(parcel, "sub", 0, 0)
    return jnp.swapaxes(got, 0, 1).reshape(2, cells, channels), parcel, k1


def per_device(
    query_maps, source_maps, hubs, pick, weight_first, bias_first, weight_second, bias_second,
    sub,
):
    chosen, parcel, k1 = gather_sources(source_maps, hubs, pick, sub, weight_first)
    correlation = scaled_corr(query_maps, chosen)
    volumes = jnp.concatenate([correlation, jnp.swapaxes(correlation, 1, 2)], axis=0)
    k2 = band_second(weight_second, parcel)
    filtered = consensus_stack(volumes, k1, k2, bias_first, bias_second)
    return (filtered[:2] + jnp.swapaxes(filtered[2:], 1, 2))[None]


def solution(mesh):
    groups, wide = mesh.shape["grp"], mesh.shape["wide"]
    sub = wide // 2
    split = jax.sharding.Mesh(mesh.devices.reshape(groups, 2, sub), ("grp", "half", "sub"))
    spread = ("grp", "half", "sub")

    def body(*args):
        return per_device(*args, sub)

    return jax.shard_map(
        body,
        mesh=split,
        in_specs=(
            P(spread, None),
            P(spread, None),
            P("grp"),
            P(spread, None),
            P(),
            P(),
            P(),
            P(),
        ),
        out_specs=P(spread, None, None, None),
        check_vma=False,
    )
```

```python
import functools

import numpy as np
import jax
import jax.numpy as jnp
from jax import lax
from jax.experimental import pallas as pl
from jax.experimental.pallas import tpu as pltpu
from jax.sharding import PartitionSpec as P

HQ = 4
WQ = 32
TAPS = 9


def band_kernel(w_ref, out_ref, *, groups):
    r = pl.program_id(0)
    cells = HQ * WQ
    row = lax.broadcasted_iota(jnp.int32, (WQ, cells), 0)
    lane = lax.broadcasted_iota(jnp.int32, (WQ, cells), 1)
    diff = row - lane % WQ + 1
    masks = [(diff == k).astype(jnp.float32) for k in range(3)]
    block = lax.broadcasted_iota(jnp.int32, (1, cells), 1) // WQ
    for g in range(groups):
        for rb in range(HQ):
            e1 = rb - block + 1
            total = None
            for k in range(3):
                wv = jnp.zeros((1, cells), jnp.float32)
                for j in range(3):
                    wv = jnp.where(e1 == j, w_ref[r, (j * 3 + k) * groups + g], wv)
                term = masks[k] * wv
                total = term if total is None else total + term
            out_ref[0, rb * WQ:(rb + 1) * WQ, g * cells:(g + 1) * cells] = total.astype(out_ref.dtype)


def banded(weights):
    rows, _, groups = weights.shape
    cells = HQ * WQ
    flat = weights.astype(jnp.float32).reshape(rows, TAPS * groups)
    return pl.pallas_call(
        functools.partial(band_kernel, groups=groups),
        out_shape=jax.ShapeDtypeStruct((rows, cells, groups * cells), weights.dtype),
        grid=(rows,),
        in_specs=[pl.BlockSpec(memory_space=pltpu.SMEM)],
        out_specs=pl.BlockSpec((1, cells, groups * cells), lambda r: (r, 0, 0)),
    )(flat)


def band_weights(weight_first, weight_second, tie):
    hid = weight_first.shape[0]
    cells = HQ * WQ
    w1 = weight_first.reshape(hid, TAPS, TAPS)
    k1 = banded(jnp.transpose(w1, (1, 2, 0))).reshape(TAPS * cells, hid * cells)
    weight_second, _ = lax.optimization_barrier((weight_second, tie))
    w2 = weight_second.reshape(hid, TAPS, TAPS)
    k2 = banded(jnp.transpose(w2, (0, 2, 1))).reshape(hid * cells, TAPS * cells)
    return k1, k2


def row_shifts(x):
    cells = x.shape[1]
    pad = WQ + 1
    padded = jnp.pad(x, ((0, 0), (pad, pad), (0, 0)))
    col = np.arange(cells) % WQ
    outs = []
    for d in range(TAPS):
        d1, d2 = d // 3 - 1, d % 3 - 1
        off = d1 * WQ + d2
        part = lax.slice_in_dim(padded, pad + off, pad + off + cells, axis=1)
        valid = (col + d2 >= 0) & (col + d2 < WQ)
        outs.append(jnp.where(valid[None, :, None], part, jnp.zeros((), x.dtype)))
    return outs


def consensus_stack(volumes, k1, k2, bias_first, bias_second):
    cells = volumes.shape[1]
    hid = bias_first.shape[0]
    stacked = jnp.concatenate(row_shifts(volumes), axis=-1)
    pre = jnp.einsum("vak,kn->van", stacked, k1, preferred_element_type=jnp.float32)
    pre = pre + jnp.repeat(bias_first, cells)[None, None, :]
    hidden = jax.nn.relu(pre).astype(jnp.bfloat16)
    part = jnp.einsum("vak,kn->van", hidden, k2, preferred_element_type=jnp.float32)
    pieces = [part[:, :, d * cells:(d + 1) * cells] for d in range(TAPS)]
    shifted = []
    for d in range(TAPS):
        shifted.append(row_shifts(pieces[d])[d])
    total = shifted[0]
    for d in range(1, TAPS):
        total = total + shifted[d]
    return jax.nn.relu(total + bias_second[0])


def scaled_corr(query, sources):
    query_f = query.astype(jnp.float32)
    sources_f = sources.astype(jnp.float32)
    query_rms = jnp.sqrt(jnp.mean(query_f * query_f, axis=-1) + 1e-06)
    source_rms = jnp.sqrt(jnp.mean(sources_f * sources_f, axis=-1) + 1e-06)
    inner = jnp.einsum("ac,jbc->jab", query, sources, preferred_element_type=jnp.float32)
    scale = jnp.sqrt(jnp.float32(query.shape[1]))
    return (inner / (scale * query_rms[None, :, None] * source_rms[:, None, :])).astype(
        jnp.bfloat16
    )


def gather_sources(source_maps, hubs, pick, sub):
    cells, channels = source_maps.shape
    rows = cells // sub
    lanes = 128
    tag = jnp.zeros((sub, rows, lanes), source_maps.dtype)
    tag = tag.at[:, 0, :2].set(pick[0][None, :].astype(source_maps.dtype))
    payload = jnp.concatenate([source_maps.reshape(sub, rows, channels), tag], axis=2)
    arrived = lax.all_to_all(payload, "sub", 0, 0)
    chunks = arrived[:, :, :channels]
    picks = arrived[:, 0, channels:channels + 2].astype(jnp.int32)
    mine = lax.axis_index("half")
    local = chunks[hubs % sub]
    mirror = lax.ppermute(local, "half", [(0, 1), (1, 0)])
    here = (hubs // sub == mine)[:, None, None]
    named = jnp.where(here, local, mirror)
    parcel = named[picks]
    got = lax.all_to_all(parcel, "sub", 0, 0)
    return jnp.swapaxes(got, 0, 1).reshape(2, cells, channels), parcel


def per_device(
    query_maps, source_maps, hubs, pick, weight_first, bias_first, weight_second, bias_second,
    sub,
):
    chosen, parcel = gather_sources(source_maps, hubs, pick, sub)
    correlation = scaled_corr(query_maps, chosen)
    volumes = jnp.concatenate([correlation, jnp.swapaxes(correlation, 1, 2)], axis=0)
    k1, k2 = band_weights(weight_first, weight_second, parcel)
    filtered = consensus_stack(volumes, k1, k2, bias_first, bias_second)
    return (filtered[:2] + jnp.swapaxes(filtered[2:], 1, 2))[None]


def solution(mesh):
    groups, wide = mesh.shape["grp"], mesh.shape["wide"]
    sub = wide // 2
    split = jax.sharding.Mesh(mesh.devices.reshape(groups, 2, sub), ("grp", "half", "sub"))
    spread = ("grp", "half", "sub")

    def body(*args):
        return per_device(*args, sub)

    return jax.shard_map(
        body,
        mesh=split,
        in_specs=(
            P(spread, None),
            P(spread, None),
            P("grp"),
            P(spread, None),
            P(),
            P(),
            P(),
            P(),
        ),
        out_specs=P(spread, None, None, None),
        check_vma=False,
    )
```

```python
import functools

import numpy as np
import jax
import jax.numpy as jnp
from jax import lax
from jax.experimental import pallas as pl
from jax.experimental.pallas import tpu as pltpu
from jax.sharding import PartitionSpec as P

HQ = 4
WQ = 32
TAPS = 9


def band_kernel(wv_ref, out_ref, *, groups):
    cells = HQ * WQ
    row = lax.broadcasted_iota(jnp.int32, (WQ, cells), 0)
    lane = lax.broadcasted_iota(jnp.int32, (WQ, cells), 1)
    diff = row - lane % WQ + 1
    masks = [(diff == k).astype(jnp.float32) for k in range(3)]
    for g in range(groups):
        for rb in range(HQ):
            total = None
            for k in range(3):
                term = masks[k] * wv_ref[0, rb, k, pl.ds(g, 1), :]
                total = term if total is None else total + term
            out_ref[0, rb * WQ:(rb + 1) * WQ, g * cells:(g + 1) * cells] = total.astype(out_ref.dtype)


def banded(weights):
    rows, _, groups = weights.shape
    cells = HQ * WQ
    w = weights.astype(jnp.float32).reshape(rows, 3, 3, groups)
    e1 = (np.arange(HQ)[:, None] - np.arange(cells)[None, :] // WQ + 1)[None, :, None, None, :]
    wv = jnp.zeros((rows, HQ, 3, groups, cells), jnp.float32)
    for j in range(3):
        wv = jnp.where(e1 == j, w[:, None, j, :, :, None], wv)
    return pl.pallas_call(
        functools.partial(band_kernel, groups=groups),
        out_shape=jax.ShapeDtypeStruct((rows, cells, groups * cells), weights.dtype),
        grid=(rows,),
        in_specs=[pl.BlockSpec((1, HQ, 3, groups, cells), lambda r: (r, 0, 0, 0, 0))],
        out_specs=pl.BlockSpec((1, cells, groups * cells), lambda r: (r, 0, 0)),
    )(wv)


def band_weights(weight_first, weight_second, tie):
    hid = weight_first.shape[0]
    cells = HQ * WQ
    w1 = weight_first.reshape(hid, TAPS, TAPS)
    k1 = banded(jnp.transpose(w1, (1, 2, 0))).reshape(TAPS * cells, hid * cells)
    weight_second, _ = lax.optimization_barrier((weight_second, tie))
    w2 = weight_second.reshape(hid, TAPS, TAPS)
    k2 = banded(jnp.transpose(w2, (0, 2, 1))).reshape(hid * cells, TAPS * cells)
    return k1, k2


def row_shifts(x):
    cells = x.shape[1]
    pad = WQ + 1
    padded = jnp.pad(x, ((0, 0), (pad, pad), (0, 0)))
    col = np.arange(cells) % WQ
    outs = []
    for d in range(TAPS):
        d1, d2 = d // 3 - 1, d % 3 - 1
        off = d1 * WQ + d2
        part = lax.slice_in_dim(padded, pad + off, pad + off + cells, axis=1)
        valid = (col + d2 >= 0) & (col + d2 < WQ)
        outs.append(jnp.where(valid[None, :, None], part, jnp.zeros((), x.dtype)))
    return outs


def consensus_stack(volumes, k1, k2, bias_first, bias_second):
    cells = volumes.shape[1]
    hid = bias_first.shape[0]
    stacked = jnp.concatenate(row_shifts(volumes), axis=-1)
    pre = jnp.einsum("vak,kn->van", stacked, k1, preferred_element_type=jnp.float32)
    pre = pre + jnp.repeat(bias_first, cells)[None, None, :]
    hidden = jax.nn.relu(pre).astype(jnp.bfloat16)
    part = jnp.einsum("vak,kn->van", hidden, k2, preferred_element_type=jnp.float32)
    pieces = [part[:, :, d * cells:(d + 1) * cells] for d in range(TAPS)]
    shifted = []
    for d in range(TAPS):
        shifted.append(row_shifts(pieces[d])[d])
    total = shifted[0]
    for d in range(1, TAPS):
        total = total + shifted[d]
    return jax.nn.relu(total + bias_second[0])


def scaled_corr(query, sources):
    query_f = query.astype(jnp.float32)
    sources_f = sources.astype(jnp.float32)
    query_rms = jnp.sqrt(jnp.mean(query_f * query_f, axis=-1) + 1e-06)
    source_rms = jnp.sqrt(jnp.mean(sources_f * sources_f, axis=-1) + 1e-06)
    inner = jnp.einsum("ac,jbc->jab", query, sources, preferred_element_type=jnp.float32)
    scale = jnp.sqrt(jnp.float32(query.shape[1]))
    return (inner / (scale * query_rms[None, :, None] * source_rms[:, None, :])).astype(
        jnp.bfloat16
    )


def gather_sources(source_maps, hubs, pick, sub):
    cells, channels = source_maps.shape
    rows = cells // sub
    lanes = 128
    tag = jnp.zeros((sub, rows, lanes), source_maps.dtype)
    tag = tag.at[:, 0, :2].set(pick[0][None, :].astype(source_maps.dtype))
    payload = jnp.concatenate([source_maps.reshape(sub, rows, channels), tag], axis=2)
    arrived = lax.all_to_all(payload, "sub", 0, 0)
    chunks = arrived[:, :, :channels]
    picks = arrived[:, 0, channels:channels + 2].astype(jnp.int32)
    mine = lax.axis_index("half")
    local = chunks[hubs % sub]
    mirror = lax.ppermute(local, "half", [(0, 1), (1, 0)])
    here = (hubs // sub == mine)[:, None, None]
    named = jnp.where(here, local, mirror)
    parcel = named[picks]
    got = lax.all_to_all(parcel, "sub", 0, 0)
    return jnp.swapaxes(got, 0, 1).reshape(2, cells, channels), parcel


def per_device(
    query_maps, source_maps, hubs, pick, weight_first, bias_first, weight_second, bias_second,
    sub,
):
    chosen, parcel = gather_sources(source_maps, hubs, pick, sub)
    correlation = scaled_corr(query_maps, chosen)
    volumes = jnp.concatenate([correlation, jnp.swapaxes(correlation, 1, 2)], axis=0)
    k1, k2 = band_weights(weight_first, weight_second, parcel)
    filtered = consensus_stack(volumes, k1, k2, bias_first, bias_second)
    return (filtered[:2] + jnp.swapaxes(filtered[2:], 1, 2))[None]


def solution(mesh):
    groups, wide = mesh.shape["grp"], mesh.shape["wide"]
    sub = wide // 2
    split = jax.sharding.Mesh(mesh.devices.reshape(groups, 2, sub), ("grp", "half", "sub"))
    spread = ("grp", "half", "sub")

    def body(*args):
        return per_device(*args, sub)

    return jax.shard_map(
        body,
        mesh=split,
        in_specs=(
            P(spread, None),
            P(spread, None),
            P("grp"),
            P(spread, None),
            P(),
            P(),
            P(),
            P(),
        ),
        out_specs=P(spread, None, None, None),
        check_vma=False,
    )
```

```python
import numpy as np
import jax
import jax.numpy as jnp
from jax import lax
from jax.sharding import PartitionSpec as P

HQ = 4
WQ = 32
TAPS = 9


def tap_table(cells, cols):
    row = lax.broadcasted_iota(jnp.int32, (cells, cols), 0)
    col = lax.broadcasted_iota(jnp.int32, (cells, cols), 1) % cells
    e1 = row // WQ - col // WQ + 1
    e2 = row % WQ - col % WQ + 1
    inside = (e1 >= 0) & (e1 < 3) & (e2 >= 0) & (e2 < 3)
    return jnp.where(inside, e1 * 3 + e2, -1)


def banded(weights, table, cells):
    rows, _, groups = weights.shape
    spread_w = jnp.repeat(weights, cells, axis=2)
    band = jnp.zeros((rows, cells, groups * cells), weights.dtype)
    for e in range(TAPS):
        band = jnp.where(table[None] == e, spread_w[:, e, None, :], band)
    return band


def band_weights(weight_first, weight_second, tie):
    hid = weight_first.shape[0]
    cells = HQ * WQ
    w1 = weight_first.reshape(hid, TAPS, TAPS)
    k1 = banded(jnp.transpose(w1, (1, 2, 0)), tap_table(cells, hid * cells), cells)
    k1 = k1.reshape(TAPS * cells, hid * cells)
    table, weight_second, _ = lax.optimization_barrier(
        (tap_table(cells, TAPS * cells), weight_second, tie)
    )
    w2 = weight_second.reshape(hid, TAPS, TAPS)
    k2 = banded(jnp.transpose(w2, (0, 2, 1)), table, cells)
    k2 = k2.reshape(hid * cells, TAPS * cells)
    return k1, k2


def row_shifts(x):
    cells = x.shape[1]
    pad = WQ + 1
    padded = jnp.pad(x, ((0, 0), (pad, pad), (0, 0)))
    col = np.arange(cells) % WQ
    outs = []
    for d in range(TAPS):
        d1, d2 = d // 3 - 1, d % 3 - 1
        off = d1 * WQ + d2
        part = lax.slice_in_dim(padded, pad + off, pad + off + cells, axis=1)
        valid = (col + d2 >= 0) & (col + d2 < WQ)
        outs.append(jnp.where(valid[None, :, None], part, jnp.zeros((), x.dtype)))
    return outs


def consensus_stack(volumes, k1, k2, bias_first, bias_second):
    cells = volumes.shape[1]
    hid = bias_first.shape[0]
    stacked = jnp.concatenate(row_shifts(volumes), axis=-1)
    pre = jnp.einsum("vak,kn->van", stacked, k1, preferred_element_type=jnp.float32)
    pre = pre + jnp.repeat(bias_first, cells)[None, None, :]
    hidden = jax.nn.relu(pre).astype(jnp.bfloat16)
    part = jnp.einsum("vak,kn->van", hidden, k2, preferred_element_type=jnp.float32)
    pieces = [part[:, :, d * cells:(d + 1) * cells] for d in range(TAPS)]
    shifted = []
    for d in range(TAPS):
        shifted.append(row_shifts(pieces[d])[d])
    total = shifted[0]
    for d in range(1, TAPS):
        total = total + shifted[d]
    return jax.nn.relu(total + bias_second[0])


def scaled_corr(query, sources):
    query_f = query.astype(jnp.float32)
    sources_f = sources.astype(jnp.float32)
    query_rms = jnp.sqrt(jnp.mean(query_f * query_f, axis=-1) + 1e-06)
    source_rms = jnp.sqrt(jnp.mean(sources_f * sources_f, axis=-1) + 1e-06)
    inner = jnp.einsum("ac,jbc->jab", query, sources, preferred_element_type=jnp.float32)
    scale = jnp.sqrt(jnp.float32(query.shape[1]))
    return (inner / (scale * query_rms[None, :, None] * source_rms[:, None, :])).astype(
        jnp.bfloat16
    )


def gather_sources(source_maps, hubs, pick, sub):
    cells, channels = source_maps.shape
    rows = cells // sub
    lanes = 128
    tag = jnp.zeros((sub, rows, lanes), source_maps.dtype)
    tag = tag.at[:, 0, :2].set(pick[0][None, :].astype(source_maps.dtype))
    payload = jnp.concatenate([source_maps.reshape(sub, rows, channels), tag], axis=2)
    arrived = lax.all_to_all(payload, "sub", 0, 0)
    chunks = arrived[:, :, :channels]
    picks = arrived[:, 0, channels:channels + 2].astype(jnp.int32)
    mine = lax.axis_index("half")
    local = chunks[hubs % sub]
    mirror = lax.ppermute(local, "half", [(0, 1), (1, 0)])
    here = (hubs // sub == mine)[:, None, None]
    named = jnp.where(here, local, mirror)
    parcel = named[picks]
    got = lax.all_to_all(parcel, "sub", 0, 0)
    return jnp.swapaxes(got, 0, 1).reshape(2, cells, channels), local


def per_device(
    query_maps, source_maps, hubs, pick, weight_first, bias_first, weight_second, bias_second,
    sub,
):
    chosen, local = gather_sources(source_maps, hubs, pick, sub)
    correlation = scaled_corr(query_maps, chosen)
    volumes = jnp.concatenate([correlation, jnp.swapaxes(correlation, 1, 2)], axis=0)
    k1, k2 = band_weights(weight_first, weight_second, local)
    filtered = consensus_stack(volumes, k1, k2, bias_first, bias_second)
    return (filtered[:2] + jnp.swapaxes(filtered[2:], 1, 2))[None]


def solution(mesh):
    groups, wide = mesh.shape["grp"], mesh.shape["wide"]
    sub = wide // 2
    split = jax.sharding.Mesh(mesh.devices.reshape(groups, 2, sub), ("grp", "half", "sub"))
    spread = ("grp", "half", "sub")

    def body(*args):
        return per_device(*args, sub)

    return jax.shard_map(
        body,
        mesh=split,
        in_specs=(
            P(spread, None),
            P(spread, None),
            P("grp"),
            P(spread, None),
            P(),
            P(),
            P(),
            P(),
        ),
        out_specs=P(spread, None, None, None),
        check_vma=False,
    )
```

```python
import numpy as np
import jax
import jax.numpy as jnp
from jax import lax
from jax.sharding import PartitionSpec as P

HQ = 4
WQ = 32
TAPS = 9


def tap_table(cells, cols):
    row = lax.broadcasted_iota(jnp.int32, (cells, cols), 0)
    col = lax.broadcasted_iota(jnp.int32, (cells, cols), 1) % cells
    e1 = row // WQ - col // WQ + 1
    e2 = row % WQ - col % WQ + 1
    inside = (e1 >= 0) & (e1 < 3) & (e2 >= 0) & (e2 < 3)
    return jnp.where(inside, e1 * 3 + e2, -1)


def banded(weights, table, cells):
    rows, _, groups = weights.shape
    spread_w = jnp.repeat(weights, cells, axis=2)
    band = jnp.zeros((rows, cells, groups * cells), weights.dtype)
    for e in range(TAPS):
        band = jnp.where(table[None] == e, spread_w[:, e, None, :], band)
    return band


def band_weights(weight_first, weight_second, tie):
    hid = weight_first.shape[0]
    cells = HQ * WQ
    split = 5
    w1 = jnp.transpose(weight_first.reshape(hid, TAPS, TAPS), (1, 2, 0))
    k1a = banded(w1[:split], tap_table(cells, hid * cells), cells)
    k1a = k1a.reshape(split * cells, hid * cells)
    late_w1, weight_second, _ = lax.optimization_barrier((w1[split:], weight_second, tie))
    k1b = banded(late_w1, tap_table(cells, hid * cells), cells)
    k1b = k1b.reshape((TAPS - split) * cells, hid * cells)
    w2 = weight_second.reshape(hid, TAPS, TAPS)
    k2 = banded(jnp.transpose(w2, (0, 2, 1)), tap_table(cells, TAPS * cells), cells)
    k2 = k2.reshape(hid * cells, TAPS * cells)
    return (k1a, k1b), k2


def row_shifts(x):
    cells = x.shape[1]
    pad = WQ + 1
    padded = jnp.pad(x, ((0, 0), (pad, pad), (0, 0)))
    col = np.arange(cells) % WQ
    outs = []
    for d in range(TAPS):
        d1, d2 = d // 3 - 1, d % 3 - 1
        off = d1 * WQ + d2
        part = lax.slice_in_dim(padded, pad + off, pad + off + cells, axis=1)
        valid = (col + d2 >= 0) & (col + d2 < WQ)
        outs.append(jnp.where(valid[None, :, None], part, jnp.zeros((), x.dtype)))
    return outs


def consensus_stack(volumes, k1, k2, bias_first, bias_second):
    cells = volumes.shape[1]
    hid = bias_first.shape[0]
    stacked = jnp.concatenate(row_shifts(volumes), axis=-1)
    k1a, k1b = k1
    cut = k1a.shape[0]
    pre = jnp.einsum("vak,kn->van", stacked[..., :cut], k1a, preferred_element_type=jnp.float32)
    pre = pre + jnp.einsum(
        "vak,kn->van", stacked[..., cut:], k1b, preferred_element_type=jnp.float32
    )
    pre = pre + jnp.repeat(bias_first, cells)[None, None, :]
    hidden = jax.nn.relu(pre).astype(jnp.bfloat16)
    part = jnp.einsum("vak,kn->van", hidden, k2, preferred_element_type=jnp.float32)
    pieces = [part[:, :, d * cells:(d + 1) * cells] for d in range(TAPS)]
    shifted = []
    for d in range(TAPS):
        shifted.append(row_shifts(pieces[d])[d])
    total = shifted[0]
    for d in range(1, TAPS):
        total = total + shifted[d]
    return jax.nn.relu(total + bias_second[0])


def scaled_corr(query, sources):
    query_f = query.astype(jnp.float32)
    sources_f = sources.astype(jnp.float32)
    query_rms = jnp.sqrt(jnp.mean(query_f * query_f, axis=-1) + 1e-06)
    source_rms = jnp.sqrt(jnp.mean(sources_f * sources_f, axis=-1) + 1e-06)
    inner = jnp.einsum("ac,jbc->jab", query, sources, preferred_element_type=jnp.float32)
    scale = jnp.sqrt(jnp.float32(query.shape[1]))
    return (inner / (scale * query_rms[None, :, None] * source_rms[:, None, :])).astype(
        jnp.bfloat16
    )


def gather_sources(source_maps, hubs, pick, sub):
    cells, channels = source_maps.shape
    rows = cells // sub
    lanes = 128
    tag = jnp.zeros((sub, rows, lanes), source_maps.dtype)
    tag = tag.at[:, 0, :2].set(pick[0][None, :].astype(source_maps.dtype))
    payload = jnp.concatenate([source_maps.reshape(sub, rows, channels), tag], axis=2)
    arrived = lax.all_to_all(payload, "sub", 0, 0)
    chunks = arrived[:, :, :channels]
    picks = arrived[:, 0, channels:channels + 2].astype(jnp.int32)
    mine = lax.axis_index("half")
    local = chunks[hubs % sub]
    mirror = lax.ppermute(local, "half", [(0, 1), (1, 0)])
    here = (hubs // sub == mine)[:, None, None]
    named = jnp.where(here, local, mirror)
    parcel = named[picks]
    got = lax.all_to_all(parcel, "sub", 0, 0)
    return jnp.swapaxes(got, 0, 1).reshape(2, cells, channels), local


def per_device(
    query_maps, source_maps, hubs, pick, weight_first, bias_first, weight_second, bias_second,
    sub,
):
    chosen, local = gather_sources(source_maps, hubs, pick, sub)
    correlation = scaled_corr(query_maps, chosen)
    volumes = jnp.concatenate([correlation, jnp.swapaxes(correlation, 1, 2)], axis=0)
    k1, k2 = band_weights(weight_first, weight_second, local)
    filtered = consensus_stack(volumes, k1, k2, bias_first, bias_second)
    return (filtered[:2] + jnp.swapaxes(filtered[2:], 1, 2))[None]


def solution(mesh):
    groups, wide = mesh.shape["grp"], mesh.shape["wide"]
    sub = wide // 2
    split = jax.sharding.Mesh(mesh.devices.reshape(groups, 2, sub), ("grp", "half", "sub"))
    spread = ("grp", "half", "sub")

    def body(*args):
        return per_device(*args, sub)

    return jax.shard_map(
        body,
        mesh=split,
        in_specs=(
            P(spread, None),
            P(spread, None),
            P("grp"),
            P(spread, None),
            P(),
            P(),
            P(),
            P(),
        ),
        out_specs=P(spread, None, None, None),
        check_vma=False,
    )
```

```python
import numpy as np
import jax
import jax.numpy as jnp
from jax import lax
from jax.sharding import PartitionSpec as P

HQ = 4
WQ = 32
TAPS = 9


def tap_table(cells, cols):
    row = lax.broadcasted_iota(jnp.int32, (cells, cols), 0)
    col = lax.broadcasted_iota(jnp.int32, (cells, cols), 1) % cells
    e1 = row // WQ - col // WQ + 1
    e2 = row % WQ - col % WQ + 1
    inside = (e1 >= 0) & (e1 < 3) & (e2 >= 0) & (e2 < 3)
    return jnp.where(inside, e1 * 3 + e2, -1)


def banded(weights, table, cells, tie=None):
    rows, _, groups = weights.shape
    masks = tuple(table == e for e in range(TAPS))
    if tie is not None:
        masks, weights, _ = lax.optimization_barrier((masks, weights, tie))
    spread_w = jnp.repeat(weights, cells, axis=2)
    band = jnp.zeros((rows, cells, groups * cells), weights.dtype)
    for e in range(TAPS):
        band = jnp.where(masks[e][None], spread_w[:, e, None, :], band)
    return band


def band_first(weight_first, tie):
    hid = weight_first.shape[0]
    cells = HQ * WQ
    w1 = weight_first.reshape(hid, TAPS, TAPS)
    k1 = banded(jnp.transpose(w1, (1, 2, 0)), tap_table(cells, hid * cells), cells, tie)
    return k1.reshape(TAPS * cells, hid * cells)


def band_second(weight_second, tie):
    hid = weight_second.shape[1]
    cells = HQ * WQ
    table, weight_second, _ = lax.optimization_barrier(
        (tap_table(cells, TAPS * cells), weight_second, tie)
    )
    w2 = weight_second.reshape(hid, TAPS, TAPS)
    k2 = banded(jnp.transpose(w2, (0, 2, 1)), table, cells)
    return k2.reshape(hid * cells, TAPS * cells)


def row_shifts(x):
    cells = x.shape[1]
    pad = WQ + 1
    padded = jnp.pad(x, ((0, 0), (pad, pad), (0, 0)))
    col = np.arange(cells) % WQ
    outs = []
    for d in range(TAPS):
        d1, d2 = d // 3 - 1, d % 3 - 1
        off = d1 * WQ + d2
        part = lax.slice_in_dim(padded, pad + off, pad + off + cells, axis=1)
        valid = (col + d2 >= 0) & (col + d2 < WQ)
        outs.append(jnp.where(valid[None, :, None], part, jnp.zeros((), x.dtype)))
    return outs


def consensus_stack(volumes, k1, k2, bias_first, bias_second):
    cells = volumes.shape[1]
    hid = bias_first.shape[0]
    stacked = jnp.concatenate(row_shifts(volumes), axis=-1)
    pre = jnp.einsum("vak,kn->van", stacked, k1, preferred_element_type=jnp.float32)
    pre = pre + jnp.repeat(bias_first, cells)[None, None, :]
    hidden = jax.nn.relu(pre).astype(jnp.bfloat16)
    part = jnp.einsum("vak,kn->van", hidden, k2, preferred_element_type=jnp.float32)
    pieces = [part[:, :, d * cells:(d + 1) * cells] for d in range(TAPS)]
    shifted = []
    for d in range(TAPS):
        shifted.append(row_shifts(pieces[d])[d])
    total = shifted[0]
    for d in range(1, TAPS):
        total = total + shifted[d]
    return jax.nn.relu(total + bias_second[0])


def scaled_corr(query, sources):
    query_f = query.astype(jnp.float32)
    sources_f = sources.astype(jnp.float32)
    query_rms = jnp.sqrt(jnp.mean(query_f * query_f, axis=-1) + 1e-06)
    source_rms = jnp.sqrt(jnp.mean(sources_f * sources_f, axis=-1) + 1e-06)
    inner = jnp.einsum("ac,jbc->jab", query, sources, preferred_element_type=jnp.float32)
    scale = jnp.sqrt(jnp.float32(query.shape[1]))
    return (inner / (scale * query_rms[None, :, None] * source_rms[:, None, :])).astype(
        jnp.bfloat16
    )


def gather_sources(source_maps, hubs, pick, sub, weight_first):
    cells, channels = source_maps.shape
    rows = cells // sub
    lanes = 128
    tag = jnp.zeros((sub, rows, lanes), source_maps.dtype)
    tag = tag.at[:, 0, :2].set(pick[0][None, :].astype(source_maps.dtype))
    payload = jnp.concatenate([source_maps.reshape(sub, rows, channels), tag], axis=2)
    arrived = lax.all_to_all(payload, "sub", 0, 0)
    chunks = arrived[:, :, :channels]
    picks = arrived[:, 0, channels:channels + 2].astype(jnp.int32)
    mine = lax.axis_index("half")
    local = chunks[hubs % sub]
    mirror = lax.ppermute(local, "half", [(0, 1), (1, 0)])
    k1 = band_first(weight_first, local)
    mirror, k1 = lax.optimization_barrier((mirror, k1))
    here = (hubs // sub == mine)[:, None, None]
    named = jnp.where(here, local, mirror)
    parcel = named[picks]
    got = lax.all_to_all(parcel, "sub", 0, 0)
    return jnp.swapaxes(got, 0, 1).reshape(2, cells, channels), parcel, k1


def per_device(
    query_maps, source_maps, hubs, pick, weight_first, bias_first, weight_second, bias_second,
    sub,
):
    chosen, parcel, k1 = gather_sources(source_maps, hubs, pick, sub, weight_first)
    correlation = scaled_corr(query_maps, chosen)
    volumes = jnp.concatenate([correlation, jnp.swapaxes(correlation, 1, 2)], axis=0)
    k2 = band_second(weight_second, parcel)
    filtered = consensus_stack(volumes, k1, k2, bias_first, bias_second)
    return (filtered[:2] + jnp.swapaxes(filtered[2:], 1, 2))[None]


def solution(mesh):
    groups, wide = mesh.shape["grp"], mesh.shape["wide"]
    sub = wide // 2
    split = jax.sharding.Mesh(mesh.devices.reshape(groups, 2, sub), ("grp", "half", "sub"))
    spread = ("grp", "half", "sub")

    def body(*args):
        return per_device(*args, sub)

    return jax.shard_map(
        body,
        mesh=split,
        in_specs=(
            P(spread, None),
            P(spread, None),
            P("grp"),
            P(spread, None),
            P(),
            P(),
            P(),
            P(),
        ),
        out_specs=P(spread, None, None, None),
        check_vma=False,
    )
```

```python
import numpy as np
import jax
import jax.numpy as jnp
from jax import lax
from jax.sharding import PartitionSpec as P

HQ = 4
WQ = 32
TAPS = 9


def tap_table(cells, cols):
    row = lax.broadcasted_iota(jnp.int32, (cells, cols), 0)
    col = lax.broadcasted_iota(jnp.int32, (cells, cols), 1) % cells
    e1 = row // WQ - col // WQ + 1
    e2 = row % WQ - col % WQ + 1
    inside = (e1 >= 0) & (e1 < 3) & (e2 >= 0) & (e2 < 3)
    return jnp.where(inside, e1 * 3 + e2, -1)


def banded(weights, table, cells, tie=None):
    rows, _, groups = weights.shape
    masks = tuple(table == e for e in range(TAPS))
    if tie is not None:
        masks, weights, _ = lax.optimization_barrier((masks, weights, tie))
    spread_w = jnp.repeat(weights, cells, axis=2)
    band = jnp.zeros((rows, cells, groups * cells), weights.dtype)
    for e in range(TAPS):
        band = jnp.where(masks[e][None], spread_w[:, e, None, :], band)
    return band


def band_first(weight_first, tie):
    hid = weight_first.shape[0]
    cells = HQ * WQ
    w1 = weight_first.reshape(hid, TAPS, TAPS)
    k1 = banded(jnp.transpose(w1, (1, 2, 0)), tap_table(cells, hid * cells), cells, tie)
    return k1.reshape(TAPS * cells, hid * cells)


def band_second(weight_second, tie):
    hid = weight_second.shape[1]
    cells = HQ * WQ
    table, weight_second, _ = lax.optimization_barrier(
        (tap_table(cells, TAPS * cells), weight_second, tie)
    )
    w2 = weight_second.reshape(hid, TAPS, TAPS)
    k2 = banded(jnp.transpose(w2, (0, 2, 1)), table, cells)
    return k2.reshape(hid * cells, TAPS * cells)


def row_shifts(x):
    cells = x.shape[1]
    pad = WQ + 1
    padded = jnp.pad(x, ((0, 0), (pad, pad), (0, 0)))
    col = np.arange(cells) % WQ
    outs = []
    for d in range(TAPS):
        d1, d2 = d // 3 - 1, d % 3 - 1
        off = d1 * WQ + d2
        part = lax.slice_in_dim(padded, pad + off, pad + off + cells, axis=1)
        valid = (col + d2 >= 0) & (col + d2 < WQ)
        outs.append(jnp.where(valid[None, :, None], part, jnp.zeros((), x.dtype)))
    return outs


def consensus_stack(volumes, k1, k2, bias_first, bias_second):
    cells = volumes.shape[1]
    hid = bias_first.shape[0]
    stacked = jnp.concatenate(row_shifts(volumes), axis=-1)
    pre = jnp.einsum("vak,kn->van", stacked, k1, preferred_element_type=jnp.float32)
    pre = pre + jnp.repeat(bias_first, cells)[None, None, :]
    hidden = jax.nn.relu(pre).astype(jnp.bfloat16)
    part = jnp.einsum("vak,kn->van", hidden, k2, preferred_element_type=jnp.float32)
    pieces = [part[:, :, d * cells:(d + 1) * cells] for d in range(TAPS)]
    shifted = []
    for d in range(TAPS):
        shifted.append(row_shifts(pieces[d])[d])
    total = shifted[0]
    for d in range(1, TAPS):
        total = total + shifted[d]
    return jax.nn.relu(total + bias_second[0])


def scaled_corr(query, sources):
    query_f = query.astype(jnp.float32)
    sources_f = sources.astype(jnp.float32)
    query_rms = jnp.sqrt(jnp.mean(query_f * query_f, axis=-1) + 1e-06)
    source_rms = jnp.sqrt(jnp.mean(sources_f * sources_f, axis=-1) + 1e-06)
    inner = jnp.einsum("ac,jbc->jab", query, sources, preferred_element_type=jnp.float32)
    scale = jnp.sqrt(jnp.float32(query.shape[1]))
    return (inner / (scale * query_rms[None, :, None] * source_rms[:, None, :])).astype(
        jnp.bfloat16
    )


def gather_sources(source_maps, hubs, pick, sub, weight_first):
    cells, channels = source_maps.shape
    rows = cells // sub
    lanes = 128
    row = lax.broadcasted_iota(jnp.int32, (sub, rows, lanes), 1)
    lane = lax.broadcasted_iota(jnp.int32, (sub, rows, lanes), 2)
    value = jnp.where(lane == 0, pick[0, 0], pick[0, 1]).astype(source_maps.dtype)
    tag = jnp.where((row == 0) & (lane < 2), value, jnp.zeros((), source_maps.dtype))
    payload = jnp.concatenate([source_maps.reshape(sub, rows, channels), tag], axis=2)
    arrived = lax.all_to_all(payload, "sub", 0, 0)
    chunks = arrived[:, :, :channels]
    picks = arrived[:, 0, channels:channels + 2].astype(jnp.int32)
    mine = lax.axis_index("half")
    local = chunks[hubs % sub]
    mirror = lax.ppermute(local, "half", [(0, 1), (1, 0)])
    k1 = band_first(weight_first, local)
    mirror, k1 = lax.optimization_barrier((mirror, k1))
    here = (hubs // sub == mine)[:, None, None]
    named = jnp.where(here, local, mirror)
    parcel = named[picks]
    got = lax.all_to_all(parcel, "sub", 0, 0)
    return jnp.swapaxes(got, 0, 1).reshape(2, cells, channels), parcel, k1


def per_device(
    query_maps, source_maps, hubs, pick, weight_first, bias_first, weight_second, bias_second,
    sub,
):
    chosen, parcel, k1 = gather_sources(source_maps, hubs, pick, sub, weight_first)
    correlation = scaled_corr(query_maps, chosen)
    volumes = jnp.concatenate([correlation, jnp.swapaxes(correlation, 1, 2)], axis=0)
    k2 = band_second(weight_second, parcel)
    filtered = consensus_stack(volumes, k1, k2, bias_first, bias_second)
    return (filtered[:2] + jnp.swapaxes(filtered[2:], 1, 2))[None]


def solution(mesh):
    groups, wide = mesh.shape["grp"], mesh.shape["wide"]
    sub = wide // 2
    split = jax.sharding.Mesh(mesh.devices.reshape(groups, 2, sub), ("grp", "half", "sub"))
    spread = ("grp", "half", "sub")

    def body(*args):
        return per_device(*args, sub)

    return jax.shard_map(
        body,
        mesh=split,
        in_specs=(
            P(spread, None),
            P(spread, None),
            P("grp"),
            P(spread, None),
            P(),
            P(),
            P(),
            P(),
        ),
        out_specs=P(spread, None, None, None),
        check_vma=False,
    )
```

```python
import numpy as np
import jax
import jax.numpy as jnp
from jax import lax
from jax.experimental.layout import Layout, with_layout_constraint
from jax.sharding import PartitionSpec as P

HQ = 4
WQ = 32
TAPS = 9


def tap_table(cells, cols):
    row = lax.broadcasted_iota(jnp.int32, (cells, cols), 0)
    col = lax.broadcasted_iota(jnp.int32, (cells, cols), 1) % cells
    e1 = row // WQ - col // WQ + 1
    e2 = row % WQ - col % WQ + 1
    inside = (e1 >= 0) & (e1 < 3) & (e2 >= 0) & (e2 < 3)
    return jnp.where(inside, e1 * 3 + e2, -1)


def banded(weights, table, cells, tie=None):
    rows, _, groups = weights.shape
    masks = tuple(table == e for e in range(TAPS))
    if tie is not None:
        masks, weights, _ = lax.optimization_barrier((masks, weights, tie))
    spread_w = jnp.repeat(weights, cells, axis=2)
    band = jnp.zeros((rows, cells, groups * cells), weights.dtype)
    for e in range(TAPS):
        band = jnp.where(masks[e][None], spread_w[:, e, None, :], band)
    return band


def band_first(weight_first, tie):
    hid = weight_first.shape[0]
    cells = HQ * WQ
    w1 = weight_first.reshape(hid, TAPS, TAPS)
    k1 = banded(jnp.transpose(w1, (1, 2, 0)), tap_table(cells, hid * cells), cells, tie)
    return k1.reshape(TAPS * cells, hid * cells)


def band_second(weight_second, tie):
    hid = weight_second.shape[1]
    cells = HQ * WQ
    table, weight_second, _ = lax.optimization_barrier(
        (tap_table(cells, TAPS * cells), weight_second, tie)
    )
    w2 = weight_second.reshape(hid, TAPS, TAPS)
    k2 = banded(jnp.transpose(w2, (0, 2, 1)), table, cells)
    return k2.reshape(hid * cells, TAPS * cells)


def row_shifts(x):
    cells = x.shape[1]
    pad = WQ + 1
    padded = jnp.pad(x, ((0, 0), (pad, pad), (0, 0)))
    col = np.arange(cells) % WQ
    outs = []
    for d in range(TAPS):
        d1, d2 = d // 3 - 1, d % 3 - 1
        off = d1 * WQ + d2
        part = lax.slice_in_dim(padded, pad + off, pad + off + cells, axis=1)
        valid = (col + d2 >= 0) & (col + d2 < WQ)
        outs.append(jnp.where(valid[None, :, None], part, jnp.zeros((), x.dtype)))
    return outs


def consensus_stack(volumes, k1, k2, bias_first, bias_second):
    cells = volumes.shape[1]
    hid = bias_first.shape[0]
    stacked = jnp.concatenate(row_shifts(volumes), axis=-1)
    pre = jnp.einsum("vak,kn->van", stacked, k1, preferred_element_type=jnp.float32)
    pre = pre + jnp.repeat(bias_first, cells)[None, None, :]
    hidden = jax.nn.relu(pre).astype(jnp.bfloat16)
    part = jnp.einsum("vak,kn->van", hidden, k2, preferred_element_type=jnp.float32)
    pieces = [part[:, :, d * cells:(d + 1) * cells] for d in range(TAPS)]
    shifted = []
    for d in range(TAPS):
        shifted.append(row_shifts(pieces[d])[d])
    total = shifted[0]
    for d in range(1, TAPS):
        total = total + shifted[d]
    return jax.nn.relu(total + bias_second[0])


def scaled_corr(query, sources):
    query_f = query.astype(jnp.float32)
    sources_f = sources.astype(jnp.float32)
    query_rms = jnp.sqrt(jnp.mean(query_f * query_f, axis=-1) + 1e-06)
    source_rms = jnp.sqrt(jnp.mean(sources_f * sources_f, axis=-1) + 1e-06)
    inner = jnp.einsum("ac,jbc->jab", query, sources, preferred_element_type=jnp.float32)
    scale = jnp.sqrt(jnp.float32(query.shape[1]))
    return (inner / (scale * query_rms[None, :, None] * source_rms[:, None, :])).astype(
        jnp.bfloat16
    )


def gather_sources(source_maps, hubs, pick, sub, weight_first):
    cells, channels = source_maps.shape
    rows = cells // sub
    lanes = 128
    tag = jnp.zeros((sub, rows, lanes), source_maps.dtype)
    tag = tag.at[:, 0, :2].set(pick[0][None, :].astype(source_maps.dtype))
    payload = jnp.concatenate([source_maps.reshape(sub, rows, channels), tag], axis=2)
    arrived = lax.all_to_all(payload, "sub", 0, 0)
    chunks = arrived[:, :, :channels]
    picks = arrived[:, 0, channels:channels + 2].astype(jnp.int32)
    mine = lax.axis_index("half")
    local = chunks[hubs % sub]
    mirror = lax.ppermute(local, "half", [(0, 1), (1, 0)])
    k1 = band_first(weight_first, local)
    mirror, k1 = lax.optimization_barrier((mirror, k1))
    here = (hubs // sub == mine)[:, None, None]
    named = jnp.where(here, local, mirror)
    parcel = named[picks]
    got = lax.all_to_all(parcel, "sub", 0, 0)
    return jnp.swapaxes(got, 0, 1).reshape(2, cells, channels), parcel, k1


def per_device(
    query_maps, source_maps, hubs, pick, weight_first, bias_first, weight_second, bias_second,
    sub,
):
    chosen, parcel, k1 = gather_sources(source_maps, hubs, pick, sub, weight_first)
    correlation = scaled_corr(query_maps, chosen)
    volumes = jnp.concatenate([correlation, jnp.swapaxes(correlation, 1, 2)], axis=0)
    k2 = band_second(weight_second, parcel)
    filtered = consensus_stack(volumes, k1, k2, bias_first, bias_second)
    total = filtered[:2] + jnp.swapaxes(filtered[2:], 1, 2)
    total = with_layout_constraint(total, Layout(major_to_minor=(0, 1, 2)))
    return total[None]


def solution(mesh):
    groups, wide = mesh.shape["grp"], mesh.shape["wide"]
    sub = wide // 2
    split = jax.sharding.Mesh(mesh.devices.reshape(groups, 2, sub), ("grp", "half", "sub"))
    spread = ("grp", "half", "sub")

    def body(*args):
        return per_device(*args, sub)

    return jax.shard_map(
        body,
        mesh=split,
        in_specs=(
            P(spread, None),
            P(spread, None),
            P("grp"),
            P(spread, None),
            P(),
            P(),
            P(),
            P(),
        ),
        out_specs=P(spread, None, None, None),
        check_vma=False,
    )
```

```python
import numpy as np
import jax
import jax.numpy as jnp
from jax import lax
from jax.sharding import PartitionSpec as P

HQ = 4
WQ = 32
TAPS = 9


def tap_table(cells, cols):
    row = lax.broadcasted_iota(jnp.int32, (cells, cols), 0)
    col = lax.broadcasted_iota(jnp.int32, (cells, cols), 1) % cells
    e1 = row // WQ - col // WQ + 1
    e2 = row % WQ - col % WQ + 1
    inside = (e1 >= 0) & (e1 < 3) & (e2 >= 0) & (e2 < 3)
    return jnp.where(inside, e1 * 3 + e2, -1)


def banded(weights, table, cells, tie=None):
    rows, _, groups = weights.shape
    masks = tuple(table == e for e in range(TAPS))
    if tie is not None:
        masks, weights, _ = lax.optimization_barrier((masks, weights, tie))
    spread_w = jnp.repeat(weights, cells, axis=2)
    band = jnp.zeros((rows, cells, groups * cells), weights.dtype)
    for e in range(TAPS):
        band = jnp.where(masks[e][None], spread_w[:, e, None, :], band)
    return band


def band_first(weight_first, tie):
    hid = weight_first.shape[0]
    cells = HQ * WQ
    w1 = weight_first.reshape(hid, TAPS, TAPS)
    k1 = banded(jnp.transpose(w1, (1, 2, 0)), tap_table(cells, hid * cells), cells, tie)
    return k1.reshape(TAPS * cells, hid * cells)


def band_second(weight_second, tie):
    hid = weight_second.shape[1]
    cells = HQ * WQ
    w2 = weight_second.reshape(hid, TAPS, TAPS)
    k2 = banded(jnp.transpose(w2, (0, 2, 1)), tap_table(cells, TAPS * cells), cells, tie)
    return k2.reshape(hid * cells, TAPS * cells)


def row_shifts(x):
    cells = x.shape[1]
    pad = WQ + 1
    padded = jnp.pad(x, ((0, 0), (pad, pad), (0, 0)))
    col = np.arange(cells) % WQ
    outs = []
    for d in range(TAPS):
        d1, d2 = d // 3 - 1, d % 3 - 1
        off = d1 * WQ + d2
        part = lax.slice_in_dim(padded, pad + off, pad + off + cells, axis=1)
        valid = (col + d2 >= 0) & (col + d2 < WQ)
        outs.append(jnp.where(valid[None, :, None], part, jnp.zeros((), x.dtype)))
    return outs


def consensus_stack(volumes, k1, k2, bias_first, bias_second):
    cells = volumes.shape[1]
    hid = bias_first.shape[0]
    stacked = jnp.concatenate(row_shifts(volumes), axis=-1)
    pre = jnp.einsum("vak,kn->van", stacked, k1, preferred_element_type=jnp.float32)
    pre = pre + jnp.repeat(bias_first, cells)[None, None, :]
    hidden = jax.nn.relu(pre).astype(jnp.bfloat16)
    part = jnp.einsum("vak,kn->van", hidden, k2, preferred_element_type=jnp.float32)
    pieces = [part[:, :, d * cells:(d + 1) * cells] for d in range(TAPS)]
    shifted = []
    for d in range(TAPS):
        shifted.append(row_shifts(pieces[d])[d])
    total = shifted[0]
    for d in range(1, TAPS):
        total = total + shifted[d]
    return jax.nn.relu(total + bias_second[0])


def scaled_corr(query, sources):
    query_f = query.astype(jnp.float32)
    sources_f = sources.astype(jnp.float32)
    query_rms = jnp.sqrt(jnp.mean(query_f * query_f, axis=-1) + 1e-06)
    source_rms = jnp.sqrt(jnp.mean(sources_f * sources_f, axis=-1) + 1e-06)
    inner = jnp.einsum("ac,jbc->jab", query, sources, preferred_element_type=jnp.float32)
    scale = jnp.sqrt(jnp.float32(query.shape[1]))
    return (inner / (scale * query_rms[None, :, None] * source_rms[:, None, :])).astype(
        jnp.bfloat16
    )


def gather_sources(source_maps, hubs, pick, sub, weight_first):
    cells, channels = source_maps.shape
    rows = cells // sub
    lanes = 128
    tag = jnp.zeros((sub, rows, lanes), source_maps.dtype)
    tag = tag.at[:, 0, :2].set(pick[0][None, :].astype(source_maps.dtype))
    payload = jnp.concatenate([source_maps.reshape(sub, rows, channels), tag], axis=2)
    arrived = lax.all_to_all(payload, "sub", 0, 0)
    chunks = arrived[:, :, :channels]
    picks = arrived[:, 0, channels:channels + 2].astype(jnp.int32)
    mine = lax.axis_index("half")
    local = chunks[hubs % sub]
    mirror = lax.ppermute(local, "half", [(0, 1), (1, 0)])
    k1 = band_first(weight_first, local)
    mirror, k1 = lax.optimization_barrier((mirror, k1))
    here = (hubs // sub == mine)[:, None, None]
    named = jnp.where(here, local, mirror)
    parcel = named[picks]
    got = lax.all_to_all(parcel, "sub", 0, 0)
    return jnp.swapaxes(got, 0, 1).reshape(2, cells, channels), parcel, k1


def per_device(
    query_maps, source_maps, hubs, pick, weight_first, bias_first, weight_second, bias_second,
    sub,
):
    chosen, parcel, k1 = gather_sources(source_maps, hubs, pick, sub, weight_first)
    correlation = scaled_corr(query_maps, chosen)
    volumes = jnp.concatenate([correlation, jnp.swapaxes(correlation, 1, 2)], axis=0)
    k2 = band_second(weight_second, parcel)
    filtered = consensus_stack(volumes, k1, k2, bias_first, bias_second)
    return (filtered[:2] + jnp.swapaxes(filtered[2:], 1, 2))[None]


def solution(mesh):
    groups, wide = mesh.shape["grp"], mesh.shape["wide"]
    sub = wide // 2
    split = jax.sharding.Mesh(mesh.devices.reshape(groups, 2, sub), ("grp", "half", "sub"))
    spread = ("grp", "half", "sub")

    def body(*args):
        return per_device(*args, sub)

    return jax.shard_map(
        body,
        mesh=split,
        in_specs=(
            P(spread, None),
            P(spread, None),
            P("grp"),
            P(spread, None),
            P(),
            P(),
            P(),
            P(),
        ),
        out_specs=P(spread, None, None, None),
        check_vma=False,
    )
```
